256 devices in a mesh: seq: 16 (over z_hi, y), head: 16 (over x, z_lo, core).
Axes of the slice: x: 4, y: 4, z: 8 (z_hi: 4, z_lo: 2; z = z_hi * 2 + z_lo), core: 2. Of those that a mesh axis runs over, the one named last changes fastest.
Arguments:
- queries: bfloat16 [8192, 4096], P('seq', 'head'), may hold values from -40 to 40
- stretch_keys: bfloat16 [8192, 4096], P('seq', 'head'), may hold values from -6 to 6
- stretch_values: bfloat16 [8192, 4096], P('seq', 'head'), may hold values from -6 to 6
- segment_ids: int32 [8192], replicated, may hold values from 0 to 7, never falling along the last dimension, each value on 1 to 6144 neighbouring positions
- block_live: int32 [16, 16], replicated, may hold values 0 or 1
- out_weight: bfloat16 [4096, 7168], P('head'), may hold values from -0.09375 to 0.09375
- cache_keys: bfloat16 [4, 8192, 4096], P(None, 'seq', 'head'), may hold values from -6 to 6
- cache_values: bfloat16 [4, 8192, 4096], P(None, 'seq', 'head'), may hold values from -6 to 6
- page_table: int32 [512], replicated, may hold values from 0 to 511, as said below
Outputs:
- attn_out: bfloat16 [8192, 4096], P('seq', 'head')
- proj_out: bfloat16 [8192, 7168], P(('seq', 'head'))
- decode_keys: bfloat16 [4, 512, 16, 4096], P(None, 'seq', None, 'head')
- decode_values: bfloat16 [4, 512, 16, 4096], P(None, 'seq', None, 'head')
The draws below stay inside these ranges and needn't reach their ends.
Inputs may be any that keep to these rules, and one draw needn't show every extreme that they name: page_table holds each of 0 to 511 once; the slot s belongs to request group s // 32; each aligned run of 2 pages of one token block goes to one group, and the 16 runs of one token block go to 16 different groups.
All inputs are finite; a program needn't handle non-finite values.
Results may differ from the reference program's by a relative error of at most 0.018.
Values may be sent and summed in bfloat16 or wider, within the bound.
No kernel may reach another device: no remote copies, remote signals or barrier semaphores. Data moves between devices by JAX's collectives and lax.ppermute only.
A program may use at most 128 MiB of HBM per device.

```python
import math
import jax
import jax.numpy as jnp
import numpy as np
from jax import lax

D = 7168
HEADS = 32
HD = 128
T_DEV = 512
PAGE = 16
LAYERS_KV = 4
NBLK = 16
TOKENS = 8192
PAGES_DEV = 32
NPAGES = 512
CAP = 2
N_HEAD = 16


def drawn_pair(key):
    base_keys = jax.random.fold_in(key, 71)
    base_queries = jax.random.fold_in(key, 72)
    full_shape = (TOKENS, HEADS * HD)
    key_draw = jnp.clip(jax.random.normal(base_keys, full_shape, jnp.float32), -6.0, 6.0)
    query_draw = jnp.clip(jax.random.normal(base_queries, full_shape, jnp.float32), -6.0, 6.0)
    return (query_draw, key_draw)


def draw_queries(key, part):
    return drawn_pair(key)[0].astype(jnp.bfloat16)


def draw_stretch_keys(key, part):
    return drawn_pair(key)[1].astype(jnp.bfloat16)


def draw_page_table(key, part):
    offsets = jax.random.permutation(jax.random.fold_in(key, 81), NBLK)
    order_keys = jax.random.split(jax.random.fold_in(key, 82), NBLK)
    within = jax.vmap(lambda group_key: jax.random.permutation(group_key, PAGES_DEV))(order_keys)
    page_ids = jnp.arange(NPAGES)
    source = page_ids // PAGES_DEV
    local_idx = page_ids % PAGES_DEV
    run_idx = local_idx // CAP
    groups = (source + offsets[run_idx]) % NBLK
    slot_ids = within[groups, local_idx]
    return (groups * PAGES_DEV + slot_ids).astype(jnp.int32)


def touch_ends(entries, own_key, least, high):
    longest = entries.shape.index(max(entries.shape))
    spots = []
    for shift in (0, 1):
        where = [jax.random.randint(jax.random.fold_in(own_key, axis), (), 0, length) for axis, length in enumerate(entries.shape)]
        where[longest] = (where[longest] + shift) % entries.shape[longest]
        spots.append(tuple(where))
    return entries.at[spots[0]].set(least).at[spots[1]].set(high)


def shard_levels(key, extent, cuts, low, top_value):
    def one(position, blocks):
        draws = jax.random.uniform(jax.random.fold_in(jax.random.fold_in(key, 6), position), (blocks,), jnp.float32, low / len(cuts), top_value / len(cuts))
        return jnp.repeat(jnp.exp(draws), extent[position] // blocks).reshape((-1,) + (1,) * (len(extent) - position - 1))

    factor_of = one(*cuts[0])
    for cut in cuts[1:]:
        factor_of = factor_of * one(*cut)
    return factor_of


def length_profile(count, total, reach, lean):
    portions = [(1 << 20) // math.isqrt(rank ** lean) + 1 for rank in range(2, count + 1)]
    surplus, given = total - reach - (count - 1), [1] * (count - 1)
    while surplus > 0:
        candidates = [i for i in range(count - 1) if given[i] < reach]
        whole, budget = sum([portions[i] for i in candidates]), surplus
        for i in candidates:
            extra = min(reach - given[i], max(1, budget * portions[i] // whole), surplus)
            given[i] = given[i] + extra
            surplus = surplus - extra
    return np.array([reach] + given)


def ragged(rng, count, total, limit, lean):
    if count == 2:
        one = jax.random.randint(rng, (), max(1, total - limit), min(limit, total - 1) + 1)
        return jnp.stack([one, total - one])
    lengths = jnp.asarray(length_profile(count, total, limit, lean), jnp.int32)
    couples = (count - 1) // 2
    source_of, sink = lengths[1:1 + 2 * couples:2], lengths[2:2 + 2 * couples:2]
    slack = jnp.minimum(source_of - 1, limit - sink)
    shifted = jax.random.randint(jax.random.fold_in(rng, 1), (couples,), 0, 1 << 20) % (slack + 1)
    lengths = lengths.at[1:1 + 2 * couples:2].set(source_of - shifted).at[2:2 + 2 * couples:2].set(sink + shifted)
    return lengths[jax.random.permutation(jax.random.fold_in(rng, 2), count)]


def scatter_about(key, shape, width, bound, cuts=(), kind=jnp.bfloat16):
    result = width * jax.random.normal(key, shape, jnp.float32)
    if cuts:
        result = result * shard_levels(key, shape, cuts, -0.22, 0.18)
    return jnp.clip(result, -bound, bound).astype(kind)


def setup_inputs(seed: int = 0) -> dict:
    keys = jax.random.split(jax.random.key(seed), 10)
    return {
        "queries": draw_queries(jax.random.fold_in(keys[9], 71), 0),
        "stretch_keys": draw_stretch_keys(jax.random.fold_in(keys[9], 71), 0),
        "stretch_values": scatter_about(keys[2], (TOKENS, HEADS * HD), 1.0, 6.0, ((0, 16), (1, 16))),
        "segment_ids": jnp.searchsorted(jnp.cumsum(ragged(keys[3], 8, TOKENS, 3 * TOKENS // 4, 1)), jnp.arange(TOKENS), side="right").astype(jnp.int32),
        "block_live": touch_ends((jax.random.randint(keys[4], (NBLK, NBLK), 0, 4) < 3).astype(jnp.int32), jax.random.fold_in(keys[4], 1), 0, 1),
        "out_weight": scatter_about(keys[5], (HEADS * HD, D), (HEADS * HD) ** -0.5, 0.09375, ((0, 16),)),
        "cache_keys": scatter_about(keys[6], (LAYERS_KV, TOKENS, HEADS * HD), 1.0, 6.0, ((1, 16), (2, 16))),
        "cache_values": scatter_about(keys[7], (LAYERS_KV, TOKENS, HEADS * HD), 1.0, 6.0, ((1, 16), (2, 16))),
        "page_table": draw_page_table(jax.random.fold_in(keys[9], 71), 0),
    }


def block_allowed(q_block, k_block, segment_ids, block_live):
    query_pos = q_block * T_DEV + jnp.arange(T_DEV, dtype=jnp.int32)
    key_pos = k_block * T_DEV + jnp.arange(T_DEV, dtype=jnp.int32)
    query_seg = lax.dynamic_slice_in_dim(segment_ids, q_block * T_DEV, T_DEV)
    key_seg = lax.dynamic_slice_in_dim(segment_ids, k_block * T_DEV, T_DEV)
    block_on = (k_block == q_block) | (k_block < q_block) & (block_live[q_block, k_block] == 1)
    allowed = (query_seg[:, None] == key_seg[None, :]) & (key_pos[None, :] <= query_pos[:, None]) & block_on
    return (allowed, block_on)

def block_scores(q_rows, k_rows):
    query_f32 = q_rows.astype(jnp.float32).reshape(T_DEV, HEADS, HD)
    key_f32 = k_rows.astype(jnp.float32).reshape(T_DEV, HEADS, HD)
    scores = jnp.einsum('qhd,khd->hqk', query_f32, key_f32, precision=lax.Precision.HIGHEST)
    return scores * (1.0 / math.sqrt(HD))

def attend_rows(q_block, queries, stretch_keys, stretch_values, segment_ids, block_live):
    q_rows = lax.dynamic_slice_in_dim(queries, q_block * T_DEV, T_DEV, 0)
    block_ids = jnp.arange(NBLK, dtype=jnp.int32)

    def max_step(row_best, k_block):
        allowed, block_on = block_allowed(q_block, k_block, segment_ids, block_live)

        def compute(current):
            k_rows = lax.dynamic_slice_in_dim(stretch_keys, k_block * T_DEV, T_DEV, 0)
            scores = block_scores(q_rows, k_rows)
            masked = jnp.where(allowed[None], scores, -jnp.inf)
            return jnp.maximum(current, lax.optimization_barrier(jnp.max(masked, axis=-1)))
        return (lax.cond(block_on, compute, lambda unchanged: unchanged, row_best), None)
    row_best, _ = lax.scan(max_step, jnp.full((HEADS, T_DEV), -jnp.inf, jnp.float32), block_ids)

    def sum_step(running, k_block):
        allowed, block_on = block_allowed(q_block, k_block, segment_ids, block_live)

        def compute(current):
            numerator, weight_sum = current
            k_rows = lax.dynamic_slice_in_dim(stretch_keys, k_block * T_DEV, T_DEV, 0)
            v_rows = lax.dynamic_slice_in_dim(stretch_values, k_block * T_DEV, T_DEV, 0)
            scores = block_scores(q_rows, k_rows)
            weights = jnp.where(allowed[None], jnp.exp(scores - row_best[..., None]), jnp.float32(0.0))
            weight_sum = weight_sum + lax.optimization_barrier(jnp.sum(weights, axis=-1))
            rounded = lax.optimization_barrier(weights.astype(jnp.bfloat16)).astype(jnp.float32)
            value_f32 = v_rows.astype(jnp.float32).reshape(T_DEV, HEADS, HD)
            numerator = numerator + jnp.einsum('hqk,khd->hqd', rounded, value_f32, precision=lax.Precision.HIGHEST)
            return (numerator, weight_sum)
        return (lax.cond(block_on, compute, lambda unchanged: unchanged, running), None)
    initial = (jnp.zeros((HEADS, T_DEV, HD), jnp.float32), jnp.zeros((HEADS, T_DEV), jnp.float32))
    (numerator, weight_sum), _ = lax.scan(sum_step, initial, block_ids)
    attended = numerator / weight_sum[..., None]
    return jnp.transpose(attended, (1, 0, 2)).reshape(T_DEV, HEADS * HD).astype(jnp.bfloat16)

def reference(queries, stretch_keys, stretch_values, segment_ids, block_live, out_weight, cache_keys, cache_values, page_table):
    blocks = lax.map(lambda q_block: attend_rows(q_block, queries, stretch_keys, stretch_values, segment_ids, block_live), jnp.arange(NBLK, dtype=jnp.int32))
    attn_out = blocks.reshape(TOKENS, HEADS * HD)
    group_width = HEADS * HD // N_HEAD

    def add_group(total_sum, group_idx):
        columns = lax.dynamic_slice_in_dim(attn_out, group_idx * group_width, group_width, 1)
        weight_rows = lax.dynamic_slice_in_dim(out_weight, group_idx * group_width, group_width, 0)
        partial_value = jnp.dot(columns, weight_rows, preferred_element_type=jnp.float32)
        partial_value = lax.optimization_barrier(partial_value.astype(jnp.bfloat16)).astype(jnp.float32)
        return (total_sum + partial_value, None)
    projected, _ = lax.scan(add_group, jnp.zeros((TOKENS, D), jnp.float32), jnp.arange(N_HEAD, dtype=jnp.int32))
    proj_out = projected.astype(jnp.bfloat16)

    def placed(cache):
        paged = cache.reshape(LAYERS_KV, NPAGES, PAGE, HEADS * HD)
        return jnp.zeros_like(paged).at[:, page_table].set(paged)
    return (attn_out, proj_out, placed(cache_keys), placed(cache_values))
```

```python
import functools
import math

import jax
import jax.numpy as jnp
from jax import lax
from jax.experimental import pallas as pl
from jax.experimental.pallas import tpu as pltpu
from jax.sharding import PartitionSpec as P

HD = 128
Q_ROWS = 256


def relayout(cache_keys, cache_values, page_table):
    position = lax.axis_index("seq")
    groups = lax.axis_size("seq")
    layers, block_rows, feat_width = cache_keys.shape
    page_count = page_table.shape[0] // groups
    page_len = block_rows // page_count
    per_group = page_count // groups
    table = page_table.reshape(groups, groups, per_group)
    own = lax.dynamic_index_in_dim(table, position, 0, keepdims=False)
    run_ids = jnp.arange(groups, dtype=jnp.int32)
    goes = (own[:, 0] // page_count)[None, :] == run_ids[:, None]
    run_of = jnp.sum(jnp.where(goes, run_ids[None, :], 0), axis=1)
    send_pages = (run_of[:, None] * per_group + jnp.arange(per_group, dtype=jnp.int32)[None, :]).reshape(-1)
    both = jnp.stack([cache_keys, cache_values]).reshape(2, layers, page_count, page_len, feat_width)
    outgoing = jnp.take(both, send_pages, axis=2).reshape(2, layers, groups, per_group, page_len, feat_width)
    moved = lax.all_to_all(outgoing, "seq", split_axis=2, concat_axis=2, tiled=True)
    hit = (table[:, :, 0] // page_count) == position
    slot_of = (jnp.sum(jnp.where(hit[:, :, None], table, 0), axis=1) % page_count).reshape(-1)
    arrivals = jnp.arange(page_count, dtype=jnp.int32)
    inverse = jnp.sum(jnp.where(slot_of[None, :] == arrivals[:, None], arrivals[None, :], 0), axis=1)
    placed = jnp.take(moved.reshape(2, layers, page_count, page_len, feat_width), inverse, axis=2)
    return (placed[0], placed[1])


def attention_kernel(meta_ref, q_ref, qseg_ref, kseg_ref, k_ref, v_ref, o_ref, *, block_count, block_rows, scale):
    chunk = pl.program_id(0)
    query_block = meta_ref[block_count]
    q = q_ref[...]
    qseg = qseg_ref[...]
    rows = q.shape[0]
    qpos = query_block * block_rows + chunk * rows + lax.broadcasted_iota(jnp.int32, (rows, 1), 0)
    kiota = lax.broadcasted_iota(jnp.int32, (1, block_rows), 1)

    def scores(c):
        s = lax.dot_general(
            q, k_ref[c], (((1,), (1,)), ((), ())), preferred_element_type=jnp.float32
        ) * scale
        allowed = (qseg == kseg_ref[c]) & (c * block_rows + kiota <= qpos)
        return s, allowed

    def max_body(c, m):
        def live(m):
            s, allowed = scores(c)
            return jnp.maximum(m, jnp.max(jnp.where(allowed, s, -jnp.inf), axis=1, keepdims=True))

        return lax.cond(meta_ref[c] != 0, live, lambda m: m, m)

    m = lax.fori_loop(0, block_count, max_body, jnp.full((rows, 1), -jnp.inf, jnp.float32))

    def sum_body(c, carry):
        def live(carry):
            l, acc = carry
            s, allowed = scores(c)
            w = jnp.where(allowed, jnp.exp(s - m), 0.0)
            l = l + jnp.sum(w, axis=1, keepdims=True)
            acc = acc + jnp.dot(w.astype(jnp.bfloat16), v_ref[c], preferred_element_type=jnp.float32)
            return (l, acc)

        return lax.cond(meta_ref[c] != 0, live, lambda x: x, carry)

    initial = (jnp.zeros((rows, 1), jnp.float32), jnp.zeros((rows, q.shape[1]), jnp.float32))
    l, acc = lax.fori_loop(0, block_count, sum_body, initial)
    o_ref[...] = (acc / l).astype(o_ref.dtype)


def attend_head(meta, queries, qseg, kseg, kv, head):
    block_count, _, block_rows, width = kv.shape
    rows = queries.shape[0]
    kernel = functools.partial(
        attention_kernel, block_count=block_count, block_rows=block_rows, scale=1.0 / math.sqrt(HD)
    )
    return pl.pallas_call(
        kernel,
        grid_spec=pltpu.PrefetchScalarGridSpec(
            num_scalar_prefetch=1,
            grid=(rows // Q_ROWS,),
            in_specs=[
                pl.BlockSpec((Q_ROWS, width), lambda i, meta: (i, head)),
                pl.BlockSpec((Q_ROWS, 1), lambda i, meta: (i, 0)),
                pl.BlockSpec((block_count, 1, block_rows), lambda i, meta: (0, 0, 0)),
                pl.BlockSpec((block_count, None, block_rows, width), lambda i, meta: (0, 0, 0, 0)),
                pl.BlockSpec((block_count, None, block_rows, width), lambda i, meta: (0, 1, 0, 0)),
            ],
            out_specs=pl.BlockSpec((Q_ROWS, width), lambda i, meta: (i, 0)),
        ),
        out_shape=jax.ShapeDtypeStruct((rows, width), queries.dtype),
    )(meta, queries, qseg, kseg, kv, kv)


def attention(queries, stretch_keys, stretch_values, segment_ids, block_live):
    position = lax.axis_index("seq")
    block_count = lax.axis_size("seq")
    block_rows, feat_width = queries.shape
    head_count = feat_width // HD
    seg_blocks = segment_ids.reshape(block_count, block_rows)
    query_seg = lax.dynamic_index_in_dim(seg_blocks, position, 0, keepdims=False)
    live_row = lax.dynamic_index_in_dim(block_live, position, 0, keepdims=False)
    block_ids = jnp.arange(block_count, dtype=jnp.int32)
    live = (block_ids == position) | (
        (block_ids < position) & (live_row == 1) & (seg_blocks[:, -1] >= query_seg[0])
    )
    meta = jnp.concatenate([live.astype(jnp.int32), position.astype(jnp.int32)[None]])
    qseg = query_seg[:, None]
    kseg = seg_blocks[:, None, :]
    outs = []
    for head in range(head_count):
        columns = slice(head * HD, (head + 1) * HD)
        kv = jnp.stack([stretch_keys[:, columns], stretch_values[:, columns]])
        kv_all = lax.all_gather(kv, "seq", axis=0, tiled=False)
        outs.append(attend_head(meta, queries, qseg, kseg, kv_all, head))
    return jnp.concatenate(outs, axis=1)


def local(
    queries,
    stretch_keys,
    stretch_values,
    segment_ids,
    block_live,
    out_weight,
    cache_keys,
    cache_values,
    page_table,
):
    decode_keys, decode_values = relayout(cache_keys, cache_values, page_table)
    attended = attention(queries, stretch_keys, stretch_values, segment_ids, block_live)
    projected = lax.psum_scatter(
        jnp.dot(attended, out_weight, preferred_element_type=jnp.float32).astype(jnp.bfloat16),
        "head",
        scatter_dimension=0,
        tiled=True,
    )
    return (attended, projected, decode_keys, decode_values)


def solution(mesh):
    placed = (
        P("seq", "head"),
        P("seq", "head"),
        P("seq", "head"),
        P(),
        P(),
        P("head", None),
        P(None, "seq", "head"),
        P(None, "seq", "head"),
        P(),
    )
    return jax.shard_map(
        local,
        mesh=mesh,
        in_specs=placed,
        out_specs=(
            P("seq", "head"),
            P(("seq", "head"), None),
            P(None, "seq", None, "head"),
            P(None, "seq", None, "head"),
        ),
        check_vma=False,
    )
```

```python
import functools
import math

import jax
import jax.numpy as jnp
from jax import lax
from jax.experimental import pallas as pl
from jax.experimental.pallas import tpu as pltpu
from jax.sharding import Mesh
from jax.sharding import PartitionSpec as P

HD = 128
SEQ = ("zh", "y")
HEAD = ("x", "zl", "c")
Q_ROWS = 256


def relayout(cache_keys, cache_values, page_table):
    position = lax.axis_index(SEQ)
    groups = lax.axis_size(SEQ)
    layers, block_rows, feat_width = cache_keys.shape
    page_count = page_table.shape[0] // groups
    page_len = block_rows // page_count
    per_group = page_count // groups
    table = page_table.reshape(groups, groups, per_group)
    own = lax.dynamic_index_in_dim(table, position, 0, keepdims=False)
    run_ids = jnp.arange(groups, dtype=jnp.int32)
    goes = (own[:, 0] // page_count)[None, :] == run_ids[:, None]
    run_of = jnp.sum(jnp.where(goes, run_ids[None, :], 0), axis=1)
    send_pages = (run_of[:, None] * per_group + jnp.arange(per_group, dtype=jnp.int32)[None, :]).reshape(-1)
    both = jnp.stack([cache_keys, cache_values]).reshape(2, layers, page_count, page_len, feat_width)
    outgoing = jnp.take(both, send_pages, axis=2).reshape(2, layers, groups, per_group, page_len, feat_width)
    moved = lax.all_to_all(outgoing, SEQ, split_axis=2, concat_axis=2, tiled=True)
    hit = (table[:, :, 0] // page_count) == position
    slot_of = (jnp.sum(jnp.where(hit[:, :, None], table, 0), axis=1) % page_count).reshape(-1)
    arrivals = jnp.arange(page_count, dtype=jnp.int32)
    inverse = jnp.sum(jnp.where(slot_of[None, :] == arrivals[:, None], arrivals[None, :], 0), axis=1)
    return (moved.reshape(2, layers, page_count, page_len, feat_width), inverse)


def place_pages(moved, inverse):
    placed = jnp.take(moved, inverse, axis=2)
    return (placed[0], placed[1])


def attention_kernel(meta_ref, q_ref, qseg_ref, kseg_ref, k_ref, v_ref, o_ref, *, block_count, block_rows, scale):
    chunk = pl.program_id(0)
    query_block = meta_ref[block_count]
    q = q_ref[...]
    qseg = qseg_ref[...]
    rows = q.shape[0]
    qpos = query_block * block_rows + chunk * rows + lax.broadcasted_iota(jnp.int32, (rows, 1), 0)
    kiota = lax.broadcasted_iota(jnp.int32, (1, block_rows), 1)

    def scores(c):
        s = lax.dot_general(
            q, k_ref[c], (((1,), (1,)), ((), ())), preferred_element_type=jnp.float32
        ) * scale
        allowed = (qseg == kseg_ref[c]) & (c * block_rows + kiota <= qpos)
        return s, allowed

    def max_body(c, m):
        def live(m):
            s, allowed = scores(c)
            return jnp.maximum(m, jnp.max(jnp.where(allowed, s, -jnp.inf), axis=1, keepdims=True))

        return lax.cond(meta_ref[c] != 0, live, lambda m: m, m)

    m = lax.fori_loop(0, block_count, max_body, jnp.full((rows, 1), -jnp.inf, jnp.float32))

    def sum_body(c, carry):
        def live(carry):
            l, acc = carry
            s, allowed = scores(c)
            w = jnp.where(allowed, jnp.exp(s - m), 0.0)
            l = l + jnp.sum(w, axis=1, keepdims=True)
            acc = acc + jnp.dot(w.astype(jnp.bfloat16), v_ref[c], preferred_element_type=jnp.float32)
            return (l, acc)

        return lax.cond(meta_ref[c] != 0, live, lambda x: x, carry)

    initial = (jnp.zeros((rows, 1), jnp.float32), jnp.zeros((rows, q.shape[1]), jnp.float32))
    l, acc = lax.fori_loop(0, block_count, sum_body, initial)
    o_ref[...] = (acc / l).astype(o_ref.dtype)


def attend_head(meta, queries, qseg, kseg, kv, head):
    block_count, _, block_rows, width = kv.shape
    rows = queries.shape[0]
    kernel = functools.partial(
        attention_kernel, block_count=block_count, block_rows=block_rows, scale=1.0 / math.sqrt(HD)
    )
    return pl.pallas_call(
        kernel,
        grid_spec=pltpu.PrefetchScalarGridSpec(
            num_scalar_prefetch=1,
            grid=(rows // Q_ROWS,),
            in_specs=[
                pl.BlockSpec((Q_ROWS, width), lambda i, meta: (i, head)),
                pl.BlockSpec((Q_ROWS, 1), lambda i, meta: (i, 0)),
                pl.BlockSpec((block_count, 1, block_rows), lambda i, meta: (0, 0, 0)),
                pl.BlockSpec((block_count, None, block_rows, width), lambda i, meta: (0, 0, 0, 0)),
                pl.BlockSpec((block_count, None, block_rows, width), lambda i, meta: (0, 1, 0, 0)),
            ],
            out_specs=pl.BlockSpec((Q_ROWS, width), lambda i, meta: (i, 0)),
        ),
        out_shape=jax.ShapeDtypeStruct((rows, width), queries.dtype),
    )(meta, queries, qseg, kseg, kv, kv)


def attention(queries, stretch_keys, stretch_values, segment_ids, block_live, moved):
    position = lax.axis_index(SEQ)
    block_count = lax.axis_size(SEQ)
    block_rows, feat_width = queries.shape
    head_count = feat_width // HD
    seg_blocks = segment_ids.reshape(block_count, block_rows)
    query_seg = lax.dynamic_index_in_dim(seg_blocks, position, 0, keepdims=False)
    live_row = lax.dynamic_index_in_dim(block_live, position, 0, keepdims=False)
    block_ids = jnp.arange(block_count, dtype=jnp.int32)
    live = (block_ids == position) | (
        (block_ids < position) & (live_row == 1) & (seg_blocks[:, -1] >= query_seg[0])
    )
    meta = jnp.concatenate([live.astype(jnp.int32), position.astype(jnp.int32)[None]])
    qseg = query_seg[:, None]
    kseg = seg_blocks[:, None, :]
    outs = []
    for head in range(head_count):
        columns = slice(head * HD, (head + 1) * HD)
        kv = jnp.stack([stretch_keys[:, columns], stretch_values[:, columns]])
        kv_all = lax.all_gather(kv, SEQ, axis=0, tiled=False)
        if outs:
            moved, kv_all, outs = lax.optimization_barrier((moved, kv_all, outs))
        outs.append(attend_head(meta, queries, qseg, kseg, kv_all, head))
    return (jnp.concatenate(outs, axis=1), moved)


def local(
    queries,
    stretch_keys,
    stretch_values,
    segment_ids,
    block_live,
    out_weight,
    cache_keys,
    cache_values,
    page_table,
):
    moved, inverse = relayout(cache_keys, cache_values, page_table)
    attended, moved = attention(queries, stretch_keys, stretch_values, segment_ids, block_live, moved)
    decode_keys, decode_values = place_pages(moved, inverse)
    sizes = [lax.axis_size(name) for name in HEAD]
    rows, width = attended.shape
    share = rows // math.prod(sizes)
    order = attended.reshape(*sizes, share, width).transpose(2, 1, 0, 3, 4).reshape(rows, width)
    projected = jnp.dot(order, out_weight, preferred_element_type=jnp.float32).astype(jnp.bfloat16)
    for name in reversed(HEAD):
        projected = lax.psum_scatter(projected, name, scatter_dimension=0, tiled=True)
    return (attended, projected, decode_keys, decode_values)


def solution(mesh):
    seq_size, head_size = mesh.shape["seq"], mesh.shape["head"]
    fine = Mesh(mesh.devices.reshape(seq_size // 4, 4, head_size // 4, 2, 2), SEQ + HEAD)
    placed = (
        P(SEQ, HEAD),
        P(SEQ, HEAD),
        P(SEQ, HEAD),
        P(),
        P(),
        P(HEAD, None),
        P(None, SEQ, HEAD),
        P(None, SEQ, HEAD),
        P(),
    )
    return jax.shard_map(
        local,
        mesh=fine,
        in_specs=placed,
        out_specs=(
            P(SEQ, HEAD),
            P(SEQ + HEAD, None),
            P(None, SEQ, None, HEAD),
            P(None, SEQ, None, HEAD),
        ),
        check_vma=False,
    )
```

```python
import functools
import math

import jax
import jax.numpy as jnp
from jax import lax
from jax.experimental import pallas as pl
from jax.experimental.pallas import tpu as pltpu
from jax.sharding import Mesh
from jax.sharding import PartitionSpec as P

HD = 128
SEQ = ("zh", "y")
HEAD = ("x", "zl", "c")
Q_ROWS = 256


def relayout(cache_keys, cache_values, page_table):
    position = lax.axis_index(SEQ)
    groups = lax.axis_size(SEQ)
    layers, block_rows, feat_width = cache_keys.shape
    page_count = page_table.shape[0] // groups
    page_len = block_rows // page_count
    per_group = page_count // groups
    table = page_table.reshape(groups, groups, per_group)
    own = lax.dynamic_index_in_dim(table, position, 0, keepdims=False)
    run_ids = jnp.arange(groups, dtype=jnp.int32)
    goes = (own[:, 0] // page_count)[None, :] == run_ids[:, None]
    run_of = jnp.sum(jnp.where(goes, run_ids[None, :], 0), axis=1)
    send_pages = (run_of[:, None] * per_group + jnp.arange(per_group, dtype=jnp.int32)[None, :]).reshape(-1)
    both = jnp.stack([cache_keys, cache_values]).reshape(2, layers, page_count, page_len, feat_width)
    outgoing = jnp.take(both, send_pages, axis=2).reshape(2, layers, groups, per_group, page_len, feat_width)
    outgoing = outgoing.transpose(2, 0, 1, 3, 4, 5)
    moved = lax.all_to_all(outgoing, SEQ, split_axis=0, concat_axis=0, tiled=True)
    moved = moved.transpose(1, 2, 0, 3, 4, 5)
    hit = (table[:, :, 0] // page_count) == position
    slot_of = (jnp.sum(jnp.where(hit[:, :, None], table, 0), axis=1) % page_count).reshape(-1)
    arrivals = jnp.arange(page_count, dtype=jnp.int32)
    inverse = jnp.sum(jnp.where(slot_of[None, :] == arrivals[:, None], arrivals[None, :], 0), axis=1)
    return (moved.reshape(2, layers, page_count, page_len, feat_width), inverse)


def place_pages(moved, inverse):
    placed = jnp.take(moved, inverse, axis=2)
    return (placed[0], placed[1])


def attention_kernel(meta_ref, q_ref, qseg_ref, kseg_ref, k_ref, v_ref, o_ref, *, block_count, block_rows, scale):
    chunk = pl.program_id(0)
    query_block = meta_ref[block_count]
    q = q_ref[...]
    qseg = qseg_ref[...]
    rows = q.shape[0]
    qpos = query_block * block_rows + chunk * rows + lax.broadcasted_iota(jnp.int32, (rows, 1), 0)
    kiota = lax.broadcasted_iota(jnp.int32, (1, block_rows), 1)

    def scores(c):
        s = lax.dot_general(
            q, k_ref[c], (((1,), (1,)), ((), ())), preferred_element_type=jnp.float32
        ) * scale
        allowed = (qseg == kseg_ref[c]) & (c * block_rows + kiota <= qpos)
        return s, allowed

    def max_body(c, m):
        def live(m):
            s, allowed = scores(c)
            return jnp.maximum(m, jnp.max(jnp.where(allowed, s, -jnp.inf), axis=1, keepdims=True))

        return lax.cond(meta_ref[c] != 0, live, lambda m: m, m)

    m = lax.fori_loop(0, block_count, max_body, jnp.full((rows, 1), -jnp.inf, jnp.float32))

    def sum_body(c, carry):
        def live(carry):
            l, acc = carry
            s, allowed = scores(c)
            w = jnp.where(allowed, jnp.exp(s - m), 0.0)
            l = l + jnp.sum(w, axis=1, keepdims=True)
            acc = acc + jnp.dot(w.astype(jnp.bfloat16), v_ref[c], preferred_element_type=jnp.float32)
            return (l, acc)

        return lax.cond(meta_ref[c] != 0, live, lambda x: x, carry)

    initial = (jnp.zeros((rows, 1), jnp.float32), jnp.zeros((rows, q.shape[1]), jnp.float32))
    l, acc = lax.fori_loop(0, block_count, sum_body, initial)
    o_ref[...] = (acc / l).astype(o_ref.dtype)


def attend_head(meta, queries, qseg, kseg, kv, head):
    block_count, _, block_rows, width = kv.shape
    rows = queries.shape[0]
    kernel = functools.partial(
        attention_kernel, block_count=block_count, block_rows=block_rows, scale=1.0 / math.sqrt(HD)
    )
    return pl.pallas_call(
        kernel,
        grid_spec=pltpu.PrefetchScalarGridSpec(
            num_scalar_prefetch=1,
            grid=(rows // Q_ROWS,),
            in_specs=[
                pl.BlockSpec((Q_ROWS, width), lambda i, meta: (i, head)),
                pl.BlockSpec((Q_ROWS, 1), lambda i, meta: (i, 0)),
                pl.BlockSpec((block_count, 1, block_rows), lambda i, meta: (0, 0, 0)),
                pl.BlockSpec((block_count, None, block_rows, width), lambda i, meta: (0, 0, 0, 0)),
                pl.BlockSpec((block_count, None, block_rows, width), lambda i, meta: (0, 1, 0, 0)),
            ],
            out_specs=pl.BlockSpec((Q_ROWS, width), lambda i, meta: (i, 0)),
        ),
        out_shape=jax.ShapeDtypeStruct((rows, width), queries.dtype),
    )(meta, queries, qseg, kseg, kv, kv)


def attention(queries, stretch_keys, stretch_values, segment_ids, block_live, moved):
    position = lax.axis_index(SEQ)
    block_count = lax.axis_size(SEQ)
    block_rows, feat_width = queries.shape
    head_count = feat_width // HD
    seg_blocks = segment_ids.reshape(block_count, block_rows)
    query_seg = lax.dynamic_index_in_dim(seg_blocks, position, 0, keepdims=False)
    live_row = lax.dynamic_index_in_dim(block_live, position, 0, keepdims=False)
    block_ids = jnp.arange(block_count, dtype=jnp.int32)
    live = (block_ids == position) | (
        (block_ids < position) & (live_row == 1) & (seg_blocks[:, -1] >= query_seg[0])
    )
    meta = jnp.concatenate([live.astype(jnp.int32), position.astype(jnp.int32)[None]])
    qseg = query_seg[:, None]
    kseg = seg_blocks[:, None, :]
    outs = []
    for head in range(head_count):
        columns = slice(head * HD, (head + 1) * HD)
        kv = jnp.stack([stretch_keys[:, columns], stretch_values[:, columns]])
        kv_all = lax.all_gather(kv, SEQ, axis=0, tiled=False)
        if outs:
            moved, kv_all, outs = lax.optimization_barrier((moved, kv_all, outs))
        outs.append(attend_head(meta, queries, qseg, kseg, kv_all, head))
    return (jnp.concatenate(outs, axis=1), moved)


def local(
    queries,
    stretch_keys,
    stretch_values,
    segment_ids,
    block_live,
    out_weight,
    cache_keys,
    cache_values,
    page_table,
):
    moved, inverse = relayout(cache_keys, cache_values, page_table)
    attended, moved = attention(queries, stretch_keys, stretch_values, segment_ids, block_live, moved)
    decode_keys, decode_values = place_pages(moved, inverse)
    projected = reduce_rows(attended, out_weight)
    return (attended, projected, decode_keys, decode_values)


def exchange(pieces, name):
    size = pieces.shape[0]
    me = lax.axis_index(name)
    total = lax.dynamic_index_in_dim(pieces, me, 0, keepdims=False).astype(jnp.float32)
    for shift in range(1, size):
        target = (me + shift) % size
        sent = lax.dynamic_index_in_dim(pieces, target, 0, keepdims=False).astype(jnp.bfloat16)
        pairs = [(i, (i + shift) % size) for i in range(size)]
        total = total + lax.ppermute(sent, name, pairs).astype(jnp.float32)
    return total


def reduce_rows(attended, out_weight):
    x_size, zl_size, c_size = [lax.axis_size(name) for name in HEAD]
    rows, width = attended.shape
    share = rows // (x_size * zl_size * c_size)
    order = attended.reshape(x_size, zl_size, c_size, share, width).transpose(2, 0, 1, 3, 4).reshape(rows, width)
    partial = jnp.dot(order, out_weight, preferred_element_type=jnp.float32).astype(jnp.bfloat16)
    columns = partial.shape[1]
    total = exchange(partial.reshape(c_size, x_size, zl_size, share, columns), "c")
    total = exchange(total.reshape(x_size, zl_size, share, columns), "x")
    total = exchange(total.reshape(zl_size, share, columns), "zl")
    return total.astype(jnp.bfloat16)


def solution(mesh):
    seq_size, head_size = mesh.shape["seq"], mesh.shape["head"]
    fine = Mesh(mesh.devices.reshape(seq_size // 4, 4, head_size // 4, 2, 2), SEQ + HEAD)
    placed = (
        P(SEQ, HEAD),
        P(SEQ, HEAD),
        P(SEQ, HEAD),
        P(),
        P(),
        P(HEAD, None),
        P(None, SEQ, HEAD),
        P(None, SEQ, HEAD),
        P(),
    )
    return jax.shard_map(
        local,
        mesh=fine,
        in_specs=placed,
        out_specs=(
            P(SEQ, HEAD),
            P(SEQ + HEAD, None),
            P(None, SEQ, None, HEAD),
            P(None, SEQ, None, HEAD),
        ),
        check_vma=False,
    )
```

```python
import functools
import math

import jax
import jax.numpy as jnp
from jax import lax
from jax.experimental import pallas as pl
from jax.experimental.pallas import tpu as pltpu
from jax.sharding import Mesh
from jax.sharding import PartitionSpec as P

HD = 128
SEQ = ("zh", "y")
HEAD = ("x", "zl", "c")
Q_ROWS = 256


def relayout(cache_keys, cache_values, page_table):
    position = lax.axis_index(SEQ)
    groups = lax.axis_size(SEQ)
    layers, block_rows, feat_width = cache_keys.shape
    page_count = page_table.shape[0] // groups
    page_len = block_rows // page_count
    per_group = page_count // groups
    table = page_table.reshape(groups, groups, per_group)
    own = lax.dynamic_index_in_dim(table, position, 0, keepdims=False)
    run_ids = jnp.arange(groups, dtype=jnp.int32)
    goes = (own[:, 0] // page_count)[None, :] == run_ids[:, None]
    run_of = jnp.sum(jnp.where(goes, run_ids[None, :], 0), axis=1)
    send_pages = (run_of[:, None] * per_group + jnp.arange(per_group, dtype=jnp.int32)[None, :]).reshape(-1)
    both = jnp.stack([cache_keys, cache_values]).reshape(2, layers, page_count, page_len, feat_width)
    outgoing = jnp.take(both, send_pages, axis=2).reshape(2, layers, groups, per_group, page_len, feat_width)
    outgoing = outgoing.transpose(2, 0, 1, 3, 4, 5)
    hit = (table[:, :, 0] // page_count) == position
    slot_of = (jnp.sum(jnp.where(hit[:, :, None], table, 0), axis=1) % page_count).reshape(-1)
    arrivals = jnp.arange(page_count, dtype=jnp.int32)
    inverse = jnp.sum(jnp.where(slot_of[None, :] == arrivals[:, None], arrivals[None, :], 0), axis=1)
    return (outgoing, inverse)


def place_pages(outgoing, inverse):
    moved = lax.all_to_all(outgoing, SEQ, split_axis=0, concat_axis=0, tiled=True)
    _, kinds, layers, per_group, page_len, feat_width = moved.shape
    moved = moved.transpose(1, 2, 0, 3, 4, 5).reshape(kinds, layers, -1, page_len, feat_width)
    placed = jnp.take(moved, inverse, axis=2)
    return (placed[0], placed[1])


def attention_kernel(meta_ref, q_ref, qseg_ref, kseg_ref, k_ref, v_ref, o_ref, *, block_count, block_rows, scale):
    chunk = pl.program_id(0)
    query_block = meta_ref[block_count]
    q = q_ref[...]
    qseg = qseg_ref[...]
    rows = q.shape[0]
    qpos = query_block * block_rows + chunk * rows + lax.broadcasted_iota(jnp.int32, (rows, 1), 0)
    kiota = lax.broadcasted_iota(jnp.int32, (1, block_rows), 1)

    def scores(c):
        s = lax.dot_general(
            q, k_ref[c], (((1,), (1,)), ((), ())), preferred_element_type=jnp.float32
        ) * scale
        allowed = (qseg == kseg_ref[c]) & (c * block_rows + kiota <= qpos)
        return s, allowed

    def max_body(c, m):
        def live(m):
            s, allowed = scores(c)
            return jnp.maximum(m, jnp.max(jnp.where(allowed, s, -jnp.inf), axis=1, keepdims=True))

        return lax.cond(meta_ref[c] != 0, live, lambda m: m, m)

    m = lax.fori_loop(0, block_count, max_body, jnp.full((rows, 1), -jnp.inf, jnp.float32))

    def sum_body(c, carry):
        def live(carry):
            l, acc = carry
            s, allowed = scores(c)
            w = jnp.where(allowed, jnp.exp(s - m), 0.0)
            l = l + jnp.sum(w, axis=1, keepdims=True)
            acc = acc + jnp.dot(w.astype(jnp.bfloat16), v_ref[c], preferred_element_type=jnp.float32)
            return (l, acc)

        return lax.cond(meta_ref[c] != 0, live, lambda x: x, carry)

    initial = (jnp.zeros((rows, 1), jnp.float32), jnp.zeros((rows, q.shape[1]), jnp.float32))
    l, acc = lax.fori_loop(0, block_count, sum_body, initial)
    o_ref[...] = (acc / l).astype(o_ref.dtype)


def attend_head(meta, queries, qseg, kseg, kv, head):
    block_count, _, block_rows, width = kv.shape
    rows = queries.shape[0]
    kernel = functools.partial(
        attention_kernel, block_count=block_count, block_rows=block_rows, scale=1.0 / math.sqrt(HD)
    )
    return pl.pallas_call(
        kernel,
        grid_spec=pltpu.PrefetchScalarGridSpec(
            num_scalar_prefetch=1,
            grid=(rows // Q_ROWS,),
            in_specs=[
                pl.BlockSpec((Q_ROWS, width), lambda i, meta: (i, head)),
                pl.BlockSpec((Q_ROWS, 1), lambda i, meta: (i, 0)),
                pl.BlockSpec((block_count, 1, block_rows), lambda i, meta: (0, 0, 0)),
                pl.BlockSpec((block_count, None, block_rows, width), lambda i, meta: (0, 0, 0, 0)),
                pl.BlockSpec((block_count, None, block_rows, width), lambda i, meta: (0, 1, 0, 0)),
            ],
            out_specs=pl.BlockSpec((Q_ROWS, width), lambda i, meta: (i, 0)),
        ),
        out_shape=jax.ShapeDtypeStruct((rows, width), queries.dtype),
    )(meta, queries, qseg, kseg, kv, kv)


def attention(queries, stretch_keys, stretch_values, segment_ids, block_live, moved):
    position = lax.axis_index(SEQ)
    block_count = lax.axis_size(SEQ)
    block_rows, feat_width = queries.shape
    head_count = feat_width // HD
    seg_blocks = segment_ids.reshape(block_count, block_rows)
    query_seg = lax.dynamic_index_in_dim(seg_blocks, position, 0, keepdims=False)
    live_row = lax.dynamic_index_in_dim(block_live, position, 0, keepdims=False)
    block_ids = jnp.arange(block_count, dtype=jnp.int32)
    live = (block_ids == position) | (
        (block_ids < position) & (live_row == 1) & (seg_blocks[:, -1] >= query_seg[0])
    )
    meta = jnp.concatenate([live.astype(jnp.int32), position.astype(jnp.int32)[None]])
    qseg = query_seg[:, None]
    kseg = seg_blocks[:, None, :]
    outs = []
    for head in range(head_count):
        columns = slice(head * HD, (head + 1) * HD)
        kv = jnp.stack([stretch_keys[:, columns], stretch_values[:, columns]])
        kv_all = lax.all_gather(kv, SEQ, axis=0, tiled=False)
        if outs:
            moved, kv_all, outs = lax.optimization_barrier((moved, kv_all, outs))
        outs.append(attend_head(meta, queries, qseg, kseg, kv_all, head))
    return (jnp.concatenate(outs, axis=1), moved)


def local(
    queries,
    stretch_keys,
    stretch_values,
    segment_ids,
    block_live,
    out_weight,
    cache_keys,
    cache_values,
    page_table,
):
    moved, inverse = relayout(cache_keys, cache_values, page_table)
    attended, moved = attention(queries, stretch_keys, stretch_values, segment_ids, block_live, moved)
    decode_keys, decode_values = place_pages(moved, inverse)
    projected = reduce_rows(attended, out_weight)
    return (attended, projected, decode_keys, decode_values)


def exchange(pieces, name):
    size = pieces.shape[0]
    me = lax.axis_index(name)
    total = lax.dynamic_index_in_dim(pieces, me, 0, keepdims=False).astype(jnp.float32)
    for shift in range(1, size):
        target = (me + shift) % size
        sent = lax.dynamic_index_in_dim(pieces, target, 0, keepdims=False).astype(jnp.bfloat16)
        pairs = [(i, (i + shift) % size) for i in range(size)]
        total = total + lax.ppermute(sent, name, pairs).astype(jnp.float32)
    return total


def reduce_rows(attended, out_weight):
    x_size, zl_size, c_size = [lax.axis_size(name) for name in HEAD]
    rows, width = attended.shape
    share = rows // (x_size * zl_size * c_size)
    order = attended.reshape(x_size, zl_size, c_size, share, width).transpose(2, 0, 1, 3, 4).reshape(rows, width)
    partial = jnp.dot(order, out_weight, preferred_element_type=jnp.float32).astype(jnp.bfloat16)
    columns = partial.shape[1]
    total = exchange(partial.reshape(c_size, x_size, zl_size, share, columns), "c")
    total = exchange(total.reshape(x_size, zl_size, share, columns), "x")
    total = exchange(total.reshape(zl_size, share, columns), "zl")
    return total.astype(jnp.bfloat16)


def solution(mesh):
    seq_size, head_size = mesh.shape["seq"], mesh.shape["head"]
    fine = Mesh(mesh.devices.reshape(seq_size // 4, 4, head_size // 4, 2, 2), SEQ + HEAD)
    placed = (
        P(SEQ, HEAD),
        P(SEQ, HEAD),
        P(SEQ, HEAD),
        P(),
        P(),
        P(HEAD, None),
        P(None, SEQ, HEAD),
        P(None, SEQ, HEAD),
        P(),
    )
    return jax.shard_map(
        local,
        mesh=fine,
        in_specs=placed,
        out_specs=(
            P(SEQ, HEAD),
            P(SEQ + HEAD, None),
            P(None, SEQ, None, HEAD),
            P(None, SEQ, None, HEAD),
        ),
        check_vma=False,
    )
```

```python
import functools
import math

import jax
import jax.numpy as jnp
from jax import lax
from jax.experimental import pallas as pl
from jax.experimental.pallas import tpu as pltpu
from jax.sharding import Mesh
from jax.sharding import PartitionSpec as P

HD = 128
SEQ = ("zh", "y")
HEAD = ("x", "zl", "c")
Q_ROWS = 256


def relayout(cache_keys, cache_values, page_table):
    position = lax.axis_index(SEQ)
    groups = lax.axis_size(SEQ)
    layers, block_rows, feat_width = cache_keys.shape
    page_count = page_table.shape[0] // groups
    page_len = block_rows // page_count
    per_group = page_count // groups
    table = page_table.reshape(groups, groups, per_group)
    own = lax.dynamic_index_in_dim(table, position, 0, keepdims=False)
    run_ids = jnp.arange(groups, dtype=jnp.int32)
    goes = (own[:, 0] // page_count)[None, :] == run_ids[:, None]
    run_of = jnp.sum(jnp.where(goes, run_ids[None, :], 0), axis=1)
    send_pages = (run_of[:, None] * per_group + jnp.arange(per_group, dtype=jnp.int32)[None, :]).reshape(-1)
    both = jnp.stack([cache_keys, cache_values]).reshape(2, layers, page_count, page_len, feat_width)
    outgoing = jnp.take(both, send_pages, axis=2).reshape(2, layers, groups, per_group, page_len, feat_width)
    outgoing = outgoing.transpose(2, 0, 1, 3, 4, 5)
    hit = (table[:, :, 0] // page_count) == position
    slot_of = (jnp.sum(jnp.where(hit[:, :, None], table, 0), axis=1) % page_count).reshape(-1)
    arrivals = jnp.arange(page_count, dtype=jnp.int32)
    inverse = jnp.sum(jnp.where(slot_of[None, :] == arrivals[:, None], arrivals[None, :], 0), axis=1)
    return (outgoing, inverse)


def place_pages(outgoing, inverse):
    moved = lax.all_to_all(outgoing, SEQ, split_axis=0, concat_axis=0, tiled=True)
    _, kinds, layers, per_group, page_len, feat_width = moved.shape
    moved = moved.transpose(1, 2, 0, 3, 4, 5).reshape(kinds, layers, -1, page_len, feat_width)
    placed = jnp.take(moved, inverse, axis=2)
    return (placed[0], placed[1])


def attention_kernel(meta_ref, q_ref, qseg_ref, kseg_ref, k_ref, v_ref, o_ref, *, block_count, block_rows, scale):
    chunk = pl.program_id(0)
    query_block = meta_ref[block_count]
    q = q_ref[...]
    qseg = qseg_ref[...]
    rows = q.shape[0]
    qpos = query_block * block_rows + chunk * rows + lax.broadcasted_iota(jnp.int32, (rows, 1), 0)
    kiota = lax.broadcasted_iota(jnp.int32, (1, block_rows), 1)

    def scores(c):
        s = lax.dot_general(
            q, k_ref[c], (((1,), (1,)), ((), ())), preferred_element_type=jnp.float32
        ) * scale
        allowed = (qseg == kseg_ref[c]) & (c * block_rows + kiota <= qpos)
        return s, allowed

    def max_body(c, m):
        def live(m):
            s, allowed = scores(c)
            return jnp.maximum(m, jnp.max(jnp.where(allowed, s, -jnp.inf), axis=1, keepdims=True))

        return lax.cond(meta_ref[c] != 0, live, lambda m: m, m)

    m = lax.fori_loop(0, block_count, max_body, jnp.full((rows, 1), -jnp.inf, jnp.float32))

    def sum_body(c, carry):
        def live(carry):
            l, acc = carry
            s, allowed = scores(c)
            w = jnp.where(allowed, jnp.exp(s - m), 0.0)
            l = l + jnp.sum(w, axis=1, keepdims=True)
            acc = acc + jnp.dot(w.astype(jnp.bfloat16), v_ref[c], preferred_element_type=jnp.float32)
            return (l, acc)

        return lax.cond(meta_ref[c] != 0, live, lambda x: x, carry)

    initial = (jnp.zeros((rows, 1), jnp.float32), jnp.zeros((rows, q.shape[1]), jnp.float32))
    l, acc = lax.fori_loop(0, block_count, sum_body, initial)
    o_ref[...] = (acc / l).astype(o_ref.dtype)


def attend_head(meta, queries, qseg, kseg, kv, head):
    block_count, _, block_rows, _ = kv.shape
    width = HD
    rows = queries.shape[0]
    kernel = functools.partial(
        attention_kernel, block_count=block_count, block_rows=block_rows, scale=1.0 / math.sqrt(HD)
    )
    return pl.pallas_call(
        kernel,
        grid_spec=pltpu.PrefetchScalarGridSpec(
            num_scalar_prefetch=1,
            grid=(rows // Q_ROWS,),
            in_specs=[
                pl.BlockSpec((Q_ROWS, width), lambda i, meta: (i, head)),
                pl.BlockSpec((Q_ROWS, 1), lambda i, meta: (i, 0)),
                pl.BlockSpec((block_count, 1, block_rows), lambda i, meta: (0, 0, 0)),
                pl.BlockSpec((block_count, None, block_rows, width), lambda i, meta: (0, 0, 0, head)),
                pl.BlockSpec((block_count, None, block_rows, width), lambda i, meta: (0, 1, 0, head)),
            ],
            out_specs=pl.BlockSpec((Q_ROWS, width), lambda i, meta: (i, 0)),
        ),
        out_shape=jax.ShapeDtypeStruct((rows, width), queries.dtype),
    )(meta, queries, qseg, kseg, kv, kv)


def attention(queries, stretch_keys, stretch_values, segment_ids, block_live, moved):
    position = lax.axis_index(SEQ)
    block_count = lax.axis_size(SEQ)
    block_rows, feat_width = queries.shape
    head_count = feat_width // HD
    seg_blocks = segment_ids.reshape(block_count, block_rows)
    query_seg = lax.dynamic_index_in_dim(seg_blocks, position, 0, keepdims=False)
    live_row = lax.dynamic_index_in_dim(block_live, position, 0, keepdims=False)
    block_ids = jnp.arange(block_count, dtype=jnp.int32)
    live = (block_ids == position) | (
        (block_ids < position) & (live_row == 1) & (seg_blocks[:, -1] >= query_seg[0])
    )
    meta = jnp.concatenate([live.astype(jnp.int32), position.astype(jnp.int32)[None]])
    qseg = query_seg[:, None]
    kseg = seg_blocks[:, None, :]
    kv = jnp.stack([stretch_keys, stretch_values])
    kv_all = lax.all_gather(kv, SEQ, axis=0, tiled=False)
    moved, kv_all = lax.optimization_barrier((moved, kv_all))
    outs = [attend_head(meta, queries, qseg, kseg, kv_all, head) for head in range(head_count)]
    return (jnp.concatenate(outs, axis=1), moved)


def local(
    queries,
    stretch_keys,
    stretch_values,
    segment_ids,
    block_live,
    out_weight,
    cache_keys,
    cache_values,
    page_table,
):
    moved, inverse = relayout(cache_keys, cache_values, page_table)
    attended, moved = attention(queries, stretch_keys, stretch_values, segment_ids, block_live, moved)
    decode_keys, decode_values = place_pages(moved, inverse)
    projected = reduce_rows(attended, out_weight)
    return (attended, projected, decode_keys, decode_values)


def exchange(pieces, name):
    size = pieces.shape[0]
    me = lax.axis_index(name)
    total = lax.dynamic_index_in_dim(pieces, me, 0, keepdims=False).astype(jnp.float32)
    for shift in range(1, size):
        target = (me + shift) % size
        sent = lax.dynamic_index_in_dim(pieces, target, 0, keepdims=False).astype(jnp.bfloat16)
        pairs = [(i, (i + shift) % size) for i in range(size)]
        total = total + lax.ppermute(sent, name, pairs).astype(jnp.float32)
    return total


def reduce_rows(attended, out_weight):
    x_size, zl_size, c_size = [lax.axis_size(name) for name in HEAD]
    rows, width = attended.shape
    share = rows // (x_size * zl_size * c_size)
    order = attended.reshape(x_size, zl_size, c_size, share, width).transpose(2, 0, 1, 3, 4).reshape(rows, width)
    partial = jnp.dot(order, out_weight, preferred_element_type=jnp.float32).astype(jnp.bfloat16)
    columns = partial.shape[1]
    total = exchange(partial.reshape(c_size, x_size, zl_size, share, columns), "c")
    total = exchange(total.reshape(x_size, zl_size, share, columns), "x")
    total = exchange(total.reshape(zl_size, share, columns), "zl")
    return total.astype(jnp.bfloat16)


def solution(mesh):
    seq_size, head_size = mesh.shape["seq"], mesh.shape["head"]
    fine = Mesh(mesh.devices.reshape(seq_size // 4, 4, head_size // 4, 2, 2), SEQ + HEAD)
    placed = (
        P(SEQ, HEAD),
        P(SEQ, HEAD),
        P(SEQ, HEAD),
        P(),
        P(),
        P(HEAD, None),
        P(None, SEQ, HEAD),
        P(None, SEQ, HEAD),
        P(),
    )
    return jax.shard_map(
        local,
        mesh=fine,
        in_specs=placed,
        out_specs=(
            P(SEQ, HEAD),
            P(SEQ + HEAD, None),
            P(None, SEQ, None, HEAD),
            P(None, SEQ, None, HEAD),
        ),
        check_vma=False,
    )
```

```python
import functools
import math

import jax
import jax.numpy as jnp
from jax import lax
from jax.experimental import pallas as pl
from jax.experimental.pallas import tpu as pltpu
from jax.sharding import Mesh
from jax.sharding import PartitionSpec as P

HD = 128
SEQ = ("zh", "y")
HEAD = ("x", "zl", "c")
Q_ROWS = 256


def relayout(cache_keys, cache_values, page_table):
    position = lax.axis_index(SEQ)
    groups = lax.axis_size(SEQ)
    layers, block_rows, feat_width = cache_keys.shape
    page_count = page_table.shape[0] // groups
    page_len = block_rows // page_count
    per_group = page_count // groups
    table = page_table.reshape(groups, groups, per_group)
    own = lax.dynamic_index_in_dim(table, position, 0, keepdims=False)
    run_ids = jnp.arange(groups, dtype=jnp.int32)
    goes = (own[:, 0] // page_count)[None, :] == run_ids[:, None]
    run_of = jnp.sum(jnp.where(goes, run_ids[None, :], 0), axis=1)
    send_pages = (run_of[:, None] * per_group + jnp.arange(per_group, dtype=jnp.int32)[None, :]).reshape(-1)
    both = jnp.stack([cache_keys, cache_values]).reshape(2, layers, page_count, page_len, feat_width)
    outgoing = jnp.take(both, send_pages, axis=2).reshape(2, layers, groups, per_group, page_len, feat_width)
    outgoing = outgoing.transpose(2, 0, 1, 3, 4, 5)
    hit = (table[:, :, 0] // page_count) == position
    slot_of = (jnp.sum(jnp.where(hit[:, :, None], table, 0), axis=1) % page_count).reshape(-1)
    arrivals = jnp.arange(page_count, dtype=jnp.int32)
    inverse = jnp.sum(jnp.where(slot_of[None, :] == arrivals[:, None], arrivals[None, :], 0), axis=1)
    return (outgoing, inverse)


def place_pages(outgoing, inverse):
    moved = lax.all_to_all(outgoing, SEQ, split_axis=0, concat_axis=0, tiled=True)
    _, kinds, layers, per_group, page_len, feat_width = moved.shape
    moved = moved.transpose(1, 2, 0, 3, 4, 5).reshape(kinds, layers, -1, page_len, feat_width)
    placed = jnp.take(moved, inverse, axis=2)
    return (placed[0], placed[1])


def attention_kernel(meta_ref, q_ref, qseg_ref, kseg_ref, k_ref, v_ref, o_ref, *, block_count, scale):
    chunk = pl.program_id(1)
    query_block = meta_ref[block_count]
    q = q_ref[...]
    qseg = qseg_ref[...]
    rows = q.shape[0]
    block_rows = k_ref.shape[1]
    local_pos = chunk * rows + lax.broadcasted_iota(jnp.int32, (rows, 1), 0)
    key_pos = lax.broadcasted_iota(jnp.int32, (1, block_rows), 1)

    def step(c, carry, allowed):
        row_best, weight_sum, numerator = carry
        s = lax.dot_general(q, k_ref[c], (((1,), (1,)), ((), ())), preferred_element_type=jnp.float32) * scale
        if allowed is not None:
            s = jnp.where(allowed, s, -jnp.inf)
        new_best = jnp.maximum(row_best, jnp.max(s, axis=1, keepdims=True))
        rescale = jnp.exp(row_best - new_best)
        w = jnp.exp(s - new_best)
        weight_sum = rescale * weight_sum + jnp.sum(w, axis=1, keepdims=True)
        added = jnp.dot(w.astype(jnp.bfloat16), v_ref[c], preferred_element_type=jnp.float32)
        return (new_best, weight_sum, rescale * numerator + added)

    initial = (
        jnp.full((rows, 1), -jnp.inf, jnp.float32),
        jnp.zeros((rows, 1), jnp.float32),
        jnp.zeros((rows, q.shape[1]), jnp.float32),
    )
    carry = step(query_block, initial, (qseg == kseg_ref[query_block]) & (key_pos <= local_pos))

    def body(c, carry):
        flag = meta_ref[c]
        return lax.cond(
            flag == 0,
            lambda x: x,
            lambda x: lax.cond(
                flag == 1,
                lambda y: step(c, y, qseg == kseg_ref[c]),
                lambda y: step(c, y, None),
                x,
            ),
            carry,
        )

    _, weight_sum, numerator = lax.fori_loop(0, query_block, body, carry)
    o_ref[...] = (numerator / weight_sum).astype(o_ref.dtype)


def attend(meta, queries, qseg, kseg, kv):
    block_count, _, block_rows, _ = kv.shape
    rows, feat_width = queries.shape
    kernel = functools.partial(attention_kernel, block_count=block_count, scale=1.0 / math.sqrt(HD))
    return pl.pallas_call(
        kernel,
        grid_spec=pltpu.PrefetchScalarGridSpec(
            num_scalar_prefetch=1,
            grid=(feat_width // HD, rows // Q_ROWS),
            in_specs=[
                pl.BlockSpec((Q_ROWS, HD), lambda h, i, meta: (i, h)),
                pl.BlockSpec((Q_ROWS, 1), lambda h, i, meta: (i, 0)),
                pl.BlockSpec((block_count, 1, block_rows), lambda h, i, meta: (0, 0, 0)),
                pl.BlockSpec((block_count, None, block_rows, HD), lambda h, i, meta: (0, 0, 0, h)),
                pl.BlockSpec((block_count, None, block_rows, HD), lambda h, i, meta: (0, 1, 0, h)),
            ],
            out_specs=pl.BlockSpec((Q_ROWS, HD), lambda h, i, meta: (i, h)),
        ),
        out_shape=jax.ShapeDtypeStruct((rows, feat_width), queries.dtype),
    )(meta, queries, qseg, kseg, kv, kv)


def attention(queries, stretch_keys, stretch_values, segment_ids, block_live, moved):
    position = lax.axis_index(SEQ)
    block_count = lax.axis_size(SEQ)
    block_rows, feat_width = queries.shape
    head_count = feat_width // HD
    seg_blocks = segment_ids.reshape(block_count, block_rows)
    query_seg = lax.dynamic_index_in_dim(seg_blocks, position, 0, keepdims=False)
    live_row = lax.dynamic_index_in_dim(block_live, position, 0, keepdims=False)
    block_ids = jnp.arange(block_count, dtype=jnp.int32)
    earlier = (block_ids < position) & (live_row == 1) & (seg_blocks[:, -1] >= query_seg[0])
    whole = earlier & (seg_blocks[:, 0] == query_seg[-1])
    flags = jnp.where(whole, 2, jnp.where(earlier, 1, 0)).astype(jnp.int32)
    meta = jnp.concatenate([flags, position.astype(jnp.int32)[None]])
    qseg = query_seg[:, None]
    kseg = seg_blocks[:, None, :]
    kv = jnp.stack([stretch_keys, stretch_values])
    kv_all = lax.all_gather(kv, SEQ, axis=0, tiled=False)
    moved, kv_all = lax.optimization_barrier((moved, kv_all))
    return (attend(meta, queries, qseg, kseg, kv_all), moved)


def local(
    queries,
    stretch_keys,
    stretch_values,
    segment_ids,
    block_live,
    out_weight,
    cache_keys,
    cache_values,
    page_table,
):
    moved, inverse = relayout(cache_keys, cache_values, page_table)
    attended, moved = attention(queries, stretch_keys, stretch_values, segment_ids, block_live, moved)
    decode_keys, decode_values = place_pages(moved, inverse)
    projected = reduce_rows(attended, out_weight)
    return (attended, projected, decode_keys, decode_values)


def exchange(pieces, name):
    size = pieces.shape[0]
    me = lax.axis_index(name)
    total = lax.dynamic_index_in_dim(pieces, me, 0, keepdims=False).astype(jnp.float32)
    for shift in range(1, size):
        target = (me + shift) % size
        sent = lax.dynamic_index_in_dim(pieces, target, 0, keepdims=False).astype(jnp.bfloat16)
        pairs = [(i, (i + shift) % size) for i in range(size)]
        total = total + lax.ppermute(sent, name, pairs).astype(jnp.float32)
    return total


def reduce_rows(attended, out_weight):
    x_size, zl_size, c_size = [lax.axis_size(name) for name in HEAD]
    rows, width = attended.shape
    share = rows // (x_size * zl_size * c_size)
    order = attended.reshape(x_size, zl_size, c_size, share, width).transpose(2, 0, 1, 3, 4).reshape(rows, width)
    partial = jnp.dot(order, out_weight, preferred_element_type=jnp.float32).astype(jnp.bfloat16)
    columns = partial.shape[1]
    total = exchange(partial.reshape(c_size, x_size, zl_size, share, columns), "c")
    total = exchange(total.reshape(x_size, zl_size, share, columns), "x")
    total = exchange(total.reshape(zl_size, share, columns), "zl")
    return total.astype(jnp.bfloat16)


def solution(mesh):
    seq_size, head_size = mesh.shape["seq"], mesh.shape["head"]
    fine = Mesh(mesh.devices.reshape(seq_size // 4, 4, head_size // 4, 2, 2), SEQ + HEAD)
    placed = (
        P(SEQ, HEAD),
        P(SEQ, HEAD),
        P(SEQ, HEAD),
        P(),
        P(),
        P(HEAD, None),
        P(None, SEQ, HEAD),
        P(None, SEQ, HEAD),
        P(),
    )
    return jax.shard_map(
        local,
        mesh=fine,
        in_specs=placed,
        out_specs=(
            P(SEQ, HEAD),
            P(SEQ + HEAD, None),
            P(None, SEQ, None, HEAD),
            P(None, SEQ, None, HEAD),
        ),
        check_vma=False,
    )
```

```python
import functools
import math

import jax
import jax.numpy as jnp
from jax import lax
from jax.experimental import pallas as pl
from jax.experimental.pallas import tpu as pltpu
from jax.sharding import Mesh
from jax.sharding import PartitionSpec as P

HD = 128
SEQ = ("zh", "y")
HEAD = ("x", "zl", "c")
Q_ROWS = 256


def relayout(cache_keys, cache_values, page_table):
    position = lax.axis_index(SEQ)
    groups = lax.axis_size(SEQ)
    layers, block_rows, feat_width = cache_keys.shape
    page_count = page_table.shape[0] // groups
    page_len = block_rows // page_count
    per_group = page_count // groups
    table = page_table.reshape(groups, groups, per_group)
    own = lax.dynamic_index_in_dim(table, position, 0, keepdims=False)
    run_ids = jnp.arange(groups, dtype=jnp.int32)
    goes = (own[:, 0] // page_count)[None, :] == run_ids[:, None]
    run_of = jnp.sum(jnp.where(goes, run_ids[None, :], 0), axis=1)
    send_pages = (run_of[:, None] * per_group + jnp.arange(per_group, dtype=jnp.int32)[None, :]).reshape(-1)
    both = jnp.stack([cache_keys, cache_values]).reshape(2, layers, page_count, page_len, feat_width)
    outgoing = jnp.take(both, send_pages, axis=2).reshape(2, layers, groups, per_group, page_len, feat_width)
    outgoing = outgoing.transpose(2, 0, 1, 3, 4, 5)
    hit = (table[:, :, 0] // page_count) == position
    slot_of = (jnp.sum(jnp.where(hit[:, :, None], table, 0), axis=1) % page_count).reshape(-1)
    arrivals = jnp.arange(page_count, dtype=jnp.int32)
    inverse = jnp.sum(jnp.where(slot_of[None, :] == arrivals[:, None], arrivals[None, :], 0), axis=1)
    return (lax.all_to_all(outgoing, SEQ, split_axis=0, concat_axis=0, tiled=True), inverse)


def place_pages(moved, inverse):
    _, kinds, layers, per_group, page_len, feat_width = moved.shape
    moved = moved.transpose(1, 2, 0, 3, 4, 5).reshape(kinds, layers, -1, page_len, feat_width)
    placed = jnp.take(moved, inverse, axis=2)
    return (placed[0], placed[1])


def attention_kernel(meta_ref, q_ref, qseg_ref, kseg_ref, k_ref, v_ref, o_ref, *, block_count, scale):
    chunk = pl.program_id(1)
    query_block = meta_ref[block_count]
    q = q_ref[...]
    qseg = qseg_ref[...]
    rows = q.shape[0]
    block_rows = k_ref.shape[1]
    local_pos = chunk * rows + lax.broadcasted_iota(jnp.int32, (rows, 1), 0)
    key_pos = lax.broadcasted_iota(jnp.int32, (1, block_rows), 1)

    def step(c, carry, allowed):
        row_best, weight_sum, numerator = carry
        s = lax.dot_general(q, k_ref[c], (((1,), (1,)), ((), ())), preferred_element_type=jnp.float32) * scale
        if allowed is not None:
            s = jnp.where(allowed, s, -jnp.inf)
        new_best = jnp.maximum(row_best, jnp.max(s, axis=1, keepdims=True))
        rescale = jnp.exp(row_best - new_best)
        w = jnp.exp(s - new_best)
        weight_sum = rescale * weight_sum + jnp.sum(w, axis=1, keepdims=True)
        added = jnp.dot(w.astype(jnp.bfloat16), v_ref[c], preferred_element_type=jnp.float32)
        return (new_best, weight_sum, rescale * numerator + added)

    initial = (
        jnp.full((rows, 1), -jnp.inf, jnp.float32),
        jnp.zeros((rows, 1), jnp.float32),
        jnp.zeros((rows, q.shape[1]), jnp.float32),
    )
    carry = step(query_block, initial, (qseg == kseg_ref[query_block]) & (key_pos <= local_pos))

    def body(c, carry):
        flag = meta_ref[c]
        return lax.cond(
            flag == 0,
            lambda x: x,
            lambda x: lax.cond(
                flag == 1,
                lambda y: step(c, y, qseg == kseg_ref[c]),
                lambda y: step(c, y, None),
                x,
            ),
            carry,
        )

    _, weight_sum, numerator = lax.fori_loop(0, query_block, body, carry)
    o_ref[...] = (numerator / weight_sum).astype(o_ref.dtype)


def attend(meta, queries, qseg, kseg, kv):
    block_count, _, block_rows, _ = kv.shape
    rows, feat_width = queries.shape
    kernel = functools.partial(attention_kernel, block_count=block_count, scale=1.0 / math.sqrt(HD))
    return pl.pallas_call(
        kernel,
        grid_spec=pltpu.PrefetchScalarGridSpec(
            num_scalar_prefetch=1,
            grid=(feat_width // HD, rows // Q_ROWS),
            in_specs=[
                pl.BlockSpec((Q_ROWS, HD), lambda h, i, meta: (i, h)),
                pl.BlockSpec((Q_ROWS, 1), lambda h, i, meta: (i, 0)),
                pl.BlockSpec((block_count, 1, block_rows), lambda h, i, meta: (0, 0, 0)),
                pl.BlockSpec((block_count, None, block_rows, HD), lambda h, i, meta: (0, 0, 0, h)),
                pl.BlockSpec((block_count, None, block_rows, HD), lambda h, i, meta: (0, 1, 0, h)),
            ],
            out_specs=pl.BlockSpec((Q_ROWS, HD), lambda h, i, meta: (i, h)),
        ),
        out_shape=jax.ShapeDtypeStruct((rows, feat_width), queries.dtype),
    )(meta, queries, qseg, kseg, kv, kv)


def attention(queries, stretch_keys, stretch_values, segment_ids, block_live, moved):
    position = lax.axis_index(SEQ)
    block_count = lax.axis_size(SEQ)
    block_rows, feat_width = queries.shape
    head_count = feat_width // HD
    seg_blocks = segment_ids.reshape(block_count, block_rows)
    query_seg = lax.dynamic_index_in_dim(seg_blocks, position, 0, keepdims=False)
    live_row = lax.dynamic_index_in_dim(block_live, position, 0, keepdims=False)
    block_ids = jnp.arange(block_count, dtype=jnp.int32)
    earlier = (block_ids < position) & (live_row == 1) & (seg_blocks[:, -1] >= query_seg[0])
    whole = earlier & (seg_blocks[:, 0] == query_seg[-1])
    flags = jnp.where(whole, 2, jnp.where(earlier, 1, 0)).astype(jnp.int32)
    meta = jnp.concatenate([flags, position.astype(jnp.int32)[None]])
    qseg = query_seg[:, None]
    kseg = seg_blocks[:, None, :]
    kv = jnp.stack([stretch_keys, stretch_values])
    kv_all = lax.all_gather(kv, SEQ, axis=0, tiled=False)
    moved, kv_all = lax.optimization_barrier((moved, kv_all))
    return (attend(meta, queries, qseg, kseg, kv_all), moved)


def local(
    queries,
    stretch_keys,
    stretch_values,
    segment_ids,
    block_live,
    out_weight,
    cache_keys,
    cache_values,
    page_table,
):
    moved, inverse = relayout(cache_keys, cache_values, page_table)
    attended, moved = attention(queries, stretch_keys, stretch_values, segment_ids, block_live, moved)
    decode_keys, decode_values = place_pages(moved, inverse)
    projected = reduce_rows(attended, out_weight)
    return (attended, projected, decode_keys, decode_values)


def exchange(pieces, name):
    size = pieces.shape[0]
    me = lax.axis_index(name)
    total = lax.dynamic_index_in_dim(pieces, me, 0, keepdims=False).astype(jnp.float32)
    for shift in range(1, size):
        target = (me + shift) % size
        sent = lax.dynamic_index_in_dim(pieces, target, 0, keepdims=False).astype(jnp.bfloat16)
        pairs = [(i, (i + shift) % size) for i in range(size)]
        total = total + lax.ppermute(sent, name, pairs).astype(jnp.float32)
    return total


def reduce_rows(attended, out_weight):
    x_size, zl_size, c_size = [lax.axis_size(name) for name in HEAD]
    rows, width = attended.shape
    share = rows // (x_size * zl_size * c_size)
    order = attended.reshape(x_size, zl_size, c_size, share, width).transpose(2, 0, 1, 3, 4).reshape(rows, width)
    partial = jnp.dot(order, out_weight, preferred_element_type=jnp.float32).astype(jnp.bfloat16)
    columns = partial.shape[1]
    total = exchange(partial.reshape(c_size, x_size, zl_size, share, columns), "c")
    total = exchange(total.reshape(x_size, zl_size, share, columns), "x")
    total = exchange(total.reshape(zl_size, share, columns), "zl")
    return total.astype(jnp.bfloat16)


def solution(mesh):
    seq_size, head_size = mesh.shape["seq"], mesh.shape["head"]
    fine = Mesh(mesh.devices.reshape(seq_size // 4, 4, head_size // 4, 2, 2), SEQ + HEAD)
    placed = (
        P(SEQ, HEAD),
        P(SEQ, HEAD),
        P(SEQ, HEAD),
        P(),
        P(),
        P(HEAD, None),
        P(None, SEQ, HEAD),
        P(None, SEQ, HEAD),
        P(),
    )
    return jax.shard_map(
        local,
        mesh=fine,
        in_specs=placed,
        out_specs=(
            P(SEQ, HEAD),
            P(SEQ + HEAD, None),
            P(None, SEQ, None, HEAD),
            P(None, SEQ, None, HEAD),
        ),
        check_vma=False,
    )
```

```python
import functools
import math

import jax
import jax.numpy as jnp
from jax import lax
from jax.experimental import pallas as pl
from jax.experimental.pallas import tpu as pltpu
from jax.sharding import Mesh
from jax.sharding import PartitionSpec as P

HD = 128
SEQ = ("zh", "y")
HEAD = ("x", "zl", "c")
Q_ROWS = 256


def relayout(cache_keys, cache_values, page_table):
    position = lax.axis_index(SEQ)
    groups = lax.axis_size(SEQ)
    layers, block_rows, feat_width = cache_keys.shape
    page_count = page_table.shape[0] // groups
    page_len = block_rows // page_count
    per_group = page_count // groups
    table = page_table.reshape(groups, groups, per_group)
    own = lax.dynamic_index_in_dim(table, position, 0, keepdims=False)
    run_ids = jnp.arange(groups, dtype=jnp.int32)
    goes = (own[:, 0] // page_count)[None, :] == run_ids[:, None]
    run_of = jnp.sum(jnp.where(goes, run_ids[None, :], 0), axis=1)
    send_pages = (run_of[:, None] * per_group + jnp.arange(per_group, dtype=jnp.int32)[None, :]).reshape(-1)
    both = jnp.stack([cache_keys, cache_values]).reshape(2, layers, page_count, page_len, feat_width)
    outgoing = jnp.take(both, send_pages, axis=2).reshape(2, layers, groups, per_group, page_len, feat_width)
    outgoing = outgoing.transpose(2, 0, 1, 3, 4, 5)
    hit = (table[:, :, 0] // page_count) == position
    slot_by_source = jnp.sum(jnp.where(hit[:, :, None], table, 0), axis=1) % page_count
    sources = (position - run_ids) % groups
    slot_of = jnp.take(slot_by_source, sources, axis=0).reshape(-1)
    arrivals = jnp.arange(page_count, dtype=jnp.int32)
    inverse = jnp.sum(jnp.where(slot_of[None, :] == arrivals[:, None], arrivals[None, :], 0), axis=1)
    return (outgoing, inverse)


def place_pages(outgoing, inverse):
    groups = outgoing.shape[0]
    position = lax.axis_index(SEQ)
    arrived = [lax.dynamic_index_in_dim(outgoing, position, 0, keepdims=False)]
    for shift in range(1, groups):
        sent = lax.dynamic_index_in_dim(outgoing, (position + shift) % groups, 0, keepdims=False)
        pairs = [(i, (i + shift) % groups) for i in range(groups)]
        arrived.append(lax.ppermute(sent, SEQ, pairs))
    moved = jnp.stack(arrived, axis=2)
    kinds, layers, _, per_group, page_len, feat_width = moved.shape
    moved = moved.reshape(kinds, layers, -1, page_len, feat_width)
    placed = jnp.take(moved, inverse, axis=2)
    return (placed[0], placed[1])


def attention_kernel(meta_ref, q_ref, qseg_ref, kseg_ref, k_ref, v_ref, o_ref, *, block_count, scale):
    chunk = pl.program_id(1)
    query_block = meta_ref[block_count]
    q = q_ref[...]
    qseg = qseg_ref[...]
    rows = q.shape[0]
    block_rows = k_ref.shape[1]
    local_pos = chunk * rows + lax.broadcasted_iota(jnp.int32, (rows, 1), 0)
    key_pos = lax.broadcasted_iota(jnp.int32, (1, block_rows), 1)

    def step(c, carry, allowed):
        row_best, weight_sum, numerator = carry
        s = lax.dot_general(q, k_ref[c], (((1,), (1,)), ((), ())), preferred_element_type=jnp.float32) * scale
        if allowed is not None:
            s = jnp.where(allowed, s, -jnp.inf)
        new_best = jnp.maximum(row_best, jnp.max(s, axis=1, keepdims=True))
        rescale = jnp.exp(row_best - new_best)
        w = jnp.exp(s - new_best)
        weight_sum = rescale * weight_sum + jnp.sum(w, axis=1, keepdims=True)
        added = jnp.dot(w.astype(jnp.bfloat16), v_ref[c], preferred_element_type=jnp.float32)
        return (new_best, weight_sum, rescale * numerator + added)

    initial = (
        jnp.full((rows, 1), -jnp.inf, jnp.float32),
        jnp.zeros((rows, 1), jnp.float32),
        jnp.zeros((rows, q.shape[1]), jnp.float32),
    )
    carry = step(query_block, initial, (qseg == kseg_ref[query_block]) & (key_pos <= local_pos))

    def body(c, carry):
        flag = meta_ref[c]
        return lax.cond(
            flag == 0,
            lambda x: x,
            lambda x: lax.cond(
                flag == 1,
                lambda y: step(c, y, qseg == kseg_ref[c]),
                lambda y: step(c, y, None),
                x,
            ),
            carry,
        )

    _, weight_sum, numerator = lax.fori_loop(0, query_block, body, carry)
    o_ref[...] = (numerator / weight_sum).astype(o_ref.dtype)


def attend(meta, queries, qseg, kseg, kv):
    block_count, _, block_rows, _ = kv.shape
    rows, feat_width = queries.shape
    kernel = functools.partial(attention_kernel, block_count=block_count, scale=1.0 / math.sqrt(HD))
    return pl.pallas_call(
        kernel,
        grid_spec=pltpu.PrefetchScalarGridSpec(
            num_scalar_prefetch=1,
            grid=(feat_width // HD, rows // Q_ROWS),
            in_specs=[
                pl.BlockSpec((Q_ROWS, HD), lambda h, i, meta: (i, h)),
                pl.BlockSpec((Q_ROWS, 1), lambda h, i, meta: (i, 0)),
                pl.BlockSpec((block_count, 1, block_rows), lambda h, i, meta: (0, 0, 0)),
                pl.BlockSpec((block_count, None, block_rows, HD), lambda h, i, meta: (0, 0, 0, h)),
                pl.BlockSpec((block_count, None, block_rows, HD), lambda h, i, meta: (0, 1, 0, h)),
            ],
            out_specs=pl.BlockSpec((Q_ROWS, HD), lambda h, i, meta: (i, h)),
        ),
        out_shape=jax.ShapeDtypeStruct((rows, feat_width), queries.dtype),
    )(meta, queries, qseg, kseg, kv, kv)


def attention(queries, stretch_keys, stretch_values, segment_ids, block_live, moved):
    position = lax.axis_index(SEQ)
    block_count = lax.axis_size(SEQ)
    block_rows, feat_width = queries.shape
    head_count = feat_width // HD
    seg_blocks = segment_ids.reshape(block_count, block_rows)
    query_seg = lax.dynamic_index_in_dim(seg_blocks, position, 0, keepdims=False)
    live_row = lax.dynamic_index_in_dim(block_live, position, 0, keepdims=False)
    block_ids = jnp.arange(block_count, dtype=jnp.int32)
    earlier = (block_ids < position) & (live_row == 1) & (seg_blocks[:, -1] >= query_seg[0])
    whole = earlier & (seg_blocks[:, 0] == query_seg[-1])
    flags = jnp.where(whole, 2, jnp.where(earlier, 1, 0)).astype(jnp.int32)
    meta = jnp.concatenate([flags, position.astype(jnp.int32)[None]])
    qseg = query_seg[:, None]
    kseg = seg_blocks[:, None, :]
    kv = jnp.stack([stretch_keys, stretch_values])
    kv_all = lax.all_gather(kv, SEQ, axis=0, tiled=False)
    moved, kv_all = lax.optimization_barrier((moved, kv_all))
    return (attend(meta, queries, qseg, kseg, kv_all), moved)


def local(
    queries,
    stretch_keys,
    stretch_values,
    segment_ids,
    block_live,
    out_weight,
    cache_keys,
    cache_values,
    page_table,
):
    moved, inverse = relayout(cache_keys, cache_values, page_table)
    attended, moved = attention(queries, stretch_keys, stretch_values, segment_ids, block_live, moved)
    decode_keys, decode_values = place_pages(moved, inverse)
    projected = reduce_rows(attended, out_weight)
    return (attended, projected, decode_keys, decode_values)


def exchange(pieces, name):
    size = pieces.shape[0]
    me = lax.axis_index(name)
    total = lax.dynamic_index_in_dim(pieces, me, 0, keepdims=False).astype(jnp.float32)
    for shift in range(1, size):
        target = (me + shift) % size
        sent = lax.dynamic_index_in_dim(pieces, target, 0, keepdims=False).astype(jnp.bfloat16)
        pairs = [(i, (i + shift) % size) for i in range(size)]
        total = total + lax.ppermute(sent, name, pairs).astype(jnp.float32)
    return total


def reduce_rows(attended, out_weight):
    x_size, zl_size, c_size = [lax.axis_size(name) for name in HEAD]
    rows, width = attended.shape
    share = rows // (x_size * zl_size * c_size)
    order = attended.reshape(x_size, zl_size, c_size, share, width).transpose(2, 0, 1, 3, 4).reshape(rows, width)
    partial = jnp.dot(order, out_weight, preferred_element_type=jnp.float32).astype(jnp.bfloat16)
    columns = partial.shape[1]
    total = exchange(partial.reshape(c_size, x_size, zl_size, share, columns), "c")
    total = exchange(total.reshape(x_size, zl_size, share, columns), "x")
    total = exchange(total.reshape(zl_size, share, columns), "zl")
    return total.astype(jnp.bfloat16)


def solution(mesh):
    seq_size, head_size = mesh.shape["seq"], mesh.shape["head"]
    fine = Mesh(mesh.devices.reshape(seq_size // 4, 4, head_size // 4, 2, 2), SEQ + HEAD)
    placed = (
        P(SEQ, HEAD),
        P(SEQ, HEAD),
        P(SEQ, HEAD),
        P(),
        P(),
        P(HEAD, None),
        P(None, SEQ, HEAD),
        P(None, SEQ, HEAD),
        P(),
    )
    return jax.shard_map(
        local,
        mesh=fine,
        in_specs=placed,
        out_specs=(
            P(SEQ, HEAD),
            P(SEQ + HEAD, None),
            P(None, SEQ, None, HEAD),
            P(None, SEQ, None, HEAD),
        ),
        check_vma=False,
    )
```

```python
import functools
import math

import jax
import jax.numpy as jnp
from jax import lax
from jax.experimental import pallas as pl
from jax.experimental.pallas import tpu as pltpu
from jax.sharding import Mesh
from jax.sharding import PartitionSpec as P

HD = 128
SEQ = ("zh", "y")
HEAD = ("x", "zl", "c")
Q_ROWS = 256


def relayout(cache_keys, cache_values, page_table):
    position = lax.axis_index(SEQ)
    groups = lax.axis_size(SEQ)
    layers, block_rows, feat_width = cache_keys.shape
    page_count = page_table.shape[0] // groups
    page_len = block_rows // page_count
    per_group = page_count // groups
    table = page_table.reshape(groups, groups, per_group)
    own = lax.dynamic_index_in_dim(table, position, 0, keepdims=False)
    run_ids = jnp.arange(groups, dtype=jnp.int32)
    goes = (own[:, 0] // page_count)[None, :] == run_ids[:, None]
    run_of = jnp.sum(jnp.where(goes, run_ids[None, :], 0), axis=1)
    send_pages = (run_of[:, None] * per_group + jnp.arange(per_group, dtype=jnp.int32)[None, :]).reshape(-1)
    both = jnp.stack([cache_keys, cache_values]).reshape(2, layers, page_count, page_len, feat_width)
    outgoing = jnp.take(both, send_pages, axis=2).reshape(2, layers, groups, per_group, page_len, feat_width)
    outgoing = outgoing.transpose(2, 0, 1, 3, 4, 5)
    hit = (table[:, :, 0] // page_count) == position
    slot_of = (jnp.sum(jnp.where(hit[:, :, None], table, 0), axis=1) % page_count).reshape(-1)
    arrivals = jnp.arange(page_count, dtype=jnp.int32)
    inverse = jnp.sum(jnp.where(slot_of[None, :] == arrivals[:, None], arrivals[None, :], 0), axis=1)
    return (outgoing, inverse)


def place_pages(outgoing, inverse):
    moved = lax.all_to_all(outgoing, SEQ, split_axis=0, concat_axis=0, tiled=True)
    _, kinds, layers, per_group, page_len, feat_width = moved.shape
    moved = moved.transpose(1, 2, 0, 3, 4, 5).reshape(kinds, layers, -1, page_len, feat_width)
    placed = jnp.take(moved, inverse, axis=2)
    return (placed[0], placed[1])


def attention_kernel(meta_ref, q_ref, qseg_ref, kseg_ref, k_ref, v_ref, o_ref, *, block_count, scale):
    chunk = pl.program_id(1)
    query_block = meta_ref[block_count]
    q = q_ref[...]
    qseg = qseg_ref[...]
    rows = q.shape[0]
    block_rows = k_ref.shape[1]
    local_pos = chunk * rows + lax.broadcasted_iota(jnp.int32, (rows, 1), 0)
    key_pos = lax.broadcasted_iota(jnp.int32, (1, block_rows), 1)

    def step(c, carry, allowed):
        row_best, weight_sum, numerator = carry
        s = lax.dot_general(q, k_ref[c], (((1,), (1,)), ((), ())), preferred_element_type=jnp.float32) * scale
        if allowed is not None:
            s = jnp.where(allowed, s, -jnp.inf)
        new_best = jnp.maximum(row_best, jnp.max(s, axis=1, keepdims=True))
        rescale = jnp.exp(row_best - new_best)
        w = jnp.exp(s - new_best)
        weight_sum = rescale * weight_sum + jnp.sum(w, axis=1, keepdims=True)
        added = jnp.dot(w.astype(jnp.bfloat16), v_ref[c], preferred_element_type=jnp.float32)
        return (new_best, weight_sum, rescale * numerator + added)

    initial = (
        jnp.full((rows, 1), -jnp.inf, jnp.float32),
        jnp.zeros((rows, 1), jnp.float32),
        jnp.zeros((rows, q.shape[1]), jnp.float32),
    )
    carry = step(query_block, initial, (qseg == kseg_ref[query_block]) & (key_pos <= local_pos))

    def body(c, carry):
        flag = meta_ref[c]
        return lax.cond(
            flag == 0,
            lambda x: x,
            lambda x: lax.cond(
                flag == 1,
                lambda y: step(c, y, qseg == kseg_ref[c]),
                lambda y: step(c, y, None),
                x,
            ),
            carry,
        )

    _, weight_sum, numerator = lax.fori_loop(0, query_block, body, carry)
    o_ref[...] = (numerator / weight_sum).astype(o_ref.dtype)


def attend(meta, queries, qseg, kseg, kv):
    block_count, _, block_rows, _ = kv.shape
    rows, feat_width = queries.shape
    kernel = functools.partial(attention_kernel, block_count=block_count, scale=1.0 / math.sqrt(HD))
    return pl.pallas_call(
        kernel,
        grid_spec=pltpu.PrefetchScalarGridSpec(
            num_scalar_prefetch=1,
            grid=(feat_width // HD, rows // Q_ROWS),
            in_specs=[
                pl.BlockSpec((Q_ROWS, HD), lambda h, i, meta: (i, h)),
                pl.BlockSpec((Q_ROWS, 1), lambda h, i, meta: (i, 0)),
                pl.BlockSpec((block_count, 1, block_rows), lambda h, i, meta: (0, 0, 0)),
                pl.BlockSpec((block_count, None, block_rows, HD), lambda h, i, meta: (0, 0, 0, h)),
                pl.BlockSpec((block_count, None, block_rows, HD), lambda h, i, meta: (0, 1, 0, h)),
            ],
            out_specs=pl.BlockSpec((Q_ROWS, HD), lambda h, i, meta: (i, h)),
        ),
        out_shape=jax.ShapeDtypeStruct((rows, feat_width), queries.dtype),
    )(meta, queries, qseg, kseg, kv, kv)


def attention(queries, stretch_keys, stretch_values, segment_ids, block_live, moved):
    position = lax.axis_index(SEQ)
    block_count = lax.axis_size(SEQ)
    block_rows, feat_width = queries.shape
    head_count = feat_width // HD
    seg_blocks = segment_ids.reshape(block_count, block_rows)
    query_seg = lax.dynamic_index_in_dim(seg_blocks, position, 0, keepdims=False)
    live_row = lax.dynamic_index_in_dim(block_live, position, 0, keepdims=False)
    block_ids = jnp.arange(block_count, dtype=jnp.int32)
    earlier = (block_ids < position) & (live_row == 1) & (seg_blocks[:, -1] >= query_seg[0])
    whole = earlier & (seg_blocks[:, 0] == query_seg[-1])
    flags = jnp.where(whole, 2, jnp.where(earlier, 1, 0)).astype(jnp.int32)
    meta = jnp.concatenate([flags, position.astype(jnp.int32)[None]])
    qseg = query_seg[:, None]
    kseg = seg_blocks[:, None, :]
    kv = jnp.stack([stretch_keys, stretch_values])
    kv_all = lax.all_gather(kv, SEQ, axis=0, tiled=False)
    moved, kv_all = lax.optimization_barrier((moved, kv_all))
    return (attend(meta, queries, qseg, kseg, kv_all), moved)


def local(
    queries,
    stretch_keys,
    stretch_values,
    segment_ids,
    block_live,
    out_weight,
    cache_keys,
    cache_values,
    page_table,
):
    moved, inverse = relayout(cache_keys, cache_values, page_table)
    attended, moved = attention(queries, stretch_keys, stretch_values, segment_ids, block_live, moved)
    projected, moved = reduce_rows(attended, out_weight, moved)
    decode_keys, decode_values = place_pages(moved, inverse)
    return (attended, projected, decode_keys, decode_values)


def exchange(pieces, name):
    size = pieces.shape[0]
    me = lax.axis_index(name)
    total = lax.dynamic_index_in_dim(pieces, me, 0, keepdims=False).astype(jnp.float32)
    for shift in range(1, size):
        target = (me + shift) % size
        sent = lax.dynamic_index_in_dim(pieces, target, 0, keepdims=False).astype(jnp.bfloat16)
        pairs = [(i, (i + shift) % size) for i in range(size)]
        total = total + lax.ppermute(sent, name, pairs).astype(jnp.float32)
    return total


def reduce_rows(attended, out_weight, moved):
    x_size, zl_size, c_size = [lax.axis_size(name) for name in HEAD]
    rows, width = attended.shape
    share = rows // (x_size * zl_size * c_size)
    order = attended.reshape(x_size, zl_size, c_size, share, width).transpose(2, 0, 1, 3, 4).reshape(rows, width)
    partial = jnp.dot(order, out_weight, preferred_element_type=jnp.float32).astype(jnp.bfloat16)
    columns = partial.shape[1]
    total = exchange(partial.reshape(c_size, x_size, zl_size, share, columns), "c")
    total, moved = lax.optimization_barrier((total, moved))
    total = exchange(total.reshape(x_size, zl_size, share, columns), "x")
    total = exchange(total.reshape(zl_size, share, columns), "zl")
    return (total.astype(jnp.bfloat16), moved)


def solution(mesh):
    seq_size, head_size = mesh.shape["seq"], mesh.shape["head"]
    fine = Mesh(mesh.devices.reshape(seq_size // 4, 4, head_size // 4, 2, 2), SEQ + HEAD)
    placed = (
        P(SEQ, HEAD),
        P(SEQ, HEAD),
        P(SEQ, HEAD),
        P(),
        P(),
        P(HEAD, None),
        P(None, SEQ, HEAD),
        P(None, SEQ, HEAD),
        P(),
    )
    return jax.shard_map(
        local,
        mesh=fine,
        in_specs=placed,
        out_specs=(
            P(SEQ, HEAD),
            P(SEQ + HEAD, None),
            P(None, SEQ, None, HEAD),
            P(None, SEQ, None, HEAD),
        ),
        check_vma=False,
    )
```

```python
import functools
import math

import jax
import jax.numpy as jnp
from jax import lax
from jax.experimental import pallas as pl
from jax.experimental.pallas import tpu as pltpu
from jax.sharding import Mesh
from jax.sharding import PartitionSpec as P

HD = 128
SEQ = ("zh", "y")
HEAD = ("x", "zl", "c")
Q_ROWS = 512


def relayout(cache_keys, cache_values, page_table):
    position = lax.axis_index(SEQ)
    groups = lax.axis_size(SEQ)
    layers, block_rows, feat_width = cache_keys.shape
    page_count = page_table.shape[0] // groups
    page_len = block_rows // page_count
    per_group = page_count // groups
    table = page_table.reshape(groups, groups, per_group)
    own = lax.dynamic_index_in_dim(table, position, 0, keepdims=False)
    run_ids = jnp.arange(groups, dtype=jnp.int32)
    goes = (own[:, 0] // page_count)[None, :] == run_ids[:, None]
    run_of = jnp.sum(jnp.where(goes, run_ids[None, :], 0), axis=1)
    send_pages = (run_of[:, None] * per_group + jnp.arange(per_group, dtype=jnp.int32)[None, :]).reshape(-1)
    both = jnp.stack([cache_keys, cache_values]).reshape(2, layers, page_count, page_len, feat_width)
    outgoing = jnp.take(both, send_pages, axis=2).reshape(2, layers, groups, per_group, page_len, feat_width)
    outgoing = outgoing.transpose(2, 0, 1, 3, 4, 5)
    hit = (table[:, :, 0] // page_count) == position
    slot_of = (jnp.sum(jnp.where(hit[:, :, None], table, 0), axis=1) % page_count).reshape(-1)
    arrivals = jnp.arange(page_count, dtype=jnp.int32)
    inverse = jnp.sum(jnp.where(slot_of[None, :] == arrivals[:, None], arrivals[None, :], 0), axis=1)
    return (outgoing, inverse)


def place_pages(outgoing, inverse):
    moved = lax.all_to_all(outgoing, SEQ, split_axis=0, concat_axis=0, tiled=True)
    _, kinds, layers, per_group, page_len, feat_width = moved.shape
    moved = moved.transpose(1, 2, 0, 3, 4, 5).reshape(kinds, layers, -1, page_len, feat_width)
    placed = jnp.take(moved, inverse, axis=2)
    return (placed[0], placed[1])


def attention_kernel(meta_ref, q_ref, qseg_ref, kseg_ref, k_ref, v_ref, o_ref, *, block_count, scale):
    chunk = pl.program_id(1)
    query_block = meta_ref[block_count]
    q = q_ref[...]
    qseg = qseg_ref[...]
    rows = q.shape[0]
    block_rows = k_ref.shape[1]
    local_pos = chunk * rows + lax.broadcasted_iota(jnp.int32, (rows, 1), 0)
    key_pos = lax.broadcasted_iota(jnp.int32, (1, block_rows), 1)

    def step(c, carry, allowed):
        row_best, weight_sum, numerator = carry
        s = lax.dot_general(q, k_ref[c], (((1,), (1,)), ((), ())), preferred_element_type=jnp.float32) * scale
        if allowed is not None:
            s = jnp.where(allowed, s, -jnp.inf)
        new_best = jnp.maximum(row_best, jnp.max(s, axis=1, keepdims=True))
        rescale = jnp.exp(row_best - new_best)
        w = jnp.exp(s - new_best)
        weight_sum = rescale * weight_sum + jnp.sum(w, axis=1, keepdims=True)
        added = jnp.dot(w.astype(jnp.bfloat16), v_ref[c], preferred_element_type=jnp.float32)
        return (new_best, weight_sum, rescale * numerator + added)

    initial = (
        jnp.full((rows, 1), -jnp.inf, jnp.float32),
        jnp.zeros((rows, 1), jnp.float32),
        jnp.zeros((rows, q.shape[1]), jnp.float32),
    )
    carry = step(query_block, initial, (qseg == kseg_ref[query_block]) & (key_pos <= local_pos))

    def body(c, carry):
        flag = meta_ref[c]
        return lax.cond(
            flag == 0,
            lambda x: x,
            lambda x: lax.cond(
                flag == 1,
                lambda y: step(c, y, qseg == kseg_ref[c]),
                lambda y: step(c, y, None),
                x,
            ),
            carry,
        )

    _, weight_sum, numerator = lax.fori_loop(0, query_block, body, carry)
    o_ref[...] = (numerator / weight_sum).astype(o_ref.dtype)


def attend(meta, queries, qseg, kseg, kv):
    block_count, _, block_rows, _ = kv.shape
    rows, feat_width = queries.shape
    kernel = functools.partial(attention_kernel, block_count=block_count, scale=1.0 / math.sqrt(HD))
    return pl.pallas_call(
        kernel,
        grid_spec=pltpu.PrefetchScalarGridSpec(
            num_scalar_prefetch=1,
            grid=(feat_width // HD, rows // Q_ROWS),
            in_specs=[
                pl.BlockSpec((Q_ROWS, HD), lambda h, i, meta: (i, h)),
                pl.BlockSpec((Q_ROWS, 1), lambda h, i, meta: (i, 0)),
                pl.BlockSpec((block_count, 1, block_rows), lambda h, i, meta: (0, 0, 0)),
                pl.BlockSpec((block_count, None, block_rows, HD), lambda h, i, meta: (0, 0, 0, h)),
                pl.BlockSpec((block_count, None, block_rows, HD), lambda h, i, meta: (0, 1, 0, h)),
            ],
            out_specs=pl.BlockSpec((Q_ROWS, HD), lambda h, i, meta: (i, h)),
        ),
        out_shape=jax.ShapeDtypeStruct((rows, feat_width), queries.dtype),
    )(meta, queries, qseg, kseg, kv, kv)


def attention(queries, stretch_keys, stretch_values, segment_ids, block_live, moved):
    position = lax.axis_index(SEQ)
    block_count = lax.axis_size(SEQ)
    block_rows, feat_width = queries.shape
    head_count = feat_width // HD
    seg_blocks = segment_ids.reshape(block_count, block_rows)
    query_seg = lax.dynamic_index_in_dim(seg_blocks, position, 0, keepdims=False)
    live_row = lax.dynamic_index_in_dim(block_live, position, 0, keepdims=False)
    block_ids = jnp.arange(block_count, dtype=jnp.int32)
    earlier = (block_ids < position) & (live_row == 1) & (seg_blocks[:, -1] >= query_seg[0])
    whole = earlier & (seg_blocks[:, 0] == query_seg[-1])
    flags = jnp.where(whole, 2, jnp.where(earlier, 1, 0)).astype(jnp.int32)
    meta = jnp.concatenate([flags, position.astype(jnp.int32)[None]])
    qseg = query_seg[:, None]
    kseg = seg_blocks[:, None, :]
    kv = jnp.stack([stretch_keys, stretch_values])
    kv_all = lax.all_gather(kv, SEQ, axis=0, tiled=False)
    moved, kv_all = lax.optimization_barrier((moved, kv_all))
    return (attend(meta, queries, qseg, kseg, kv_all), moved)


def local(
    queries,
    stretch_keys,
    stretch_values,
    segment_ids,
    block_live,
    out_weight,
    cache_keys,
    cache_values,
    page_table,
):
    moved, inverse = relayout(cache_keys, cache_values, page_table)
    attended, moved = attention(queries, stretch_keys, stretch_values, segment_ids, block_live, moved)
    decode_keys, decode_values = place_pages(moved, inverse)
    projected = reduce_rows(attended, out_weight)
    return (attended, projected, decode_keys, decode_values)


def exchange(pieces, name):
    size = pieces.shape[0]
    me = lax.axis_index(name)
    total = lax.dynamic_index_in_dim(pieces, me, 0, keepdims=False).astype(jnp.float32)
    for shift in range(1, size):
        target = (me + shift) % size
        sent = lax.dynamic_index_in_dim(pieces, target, 0, keepdims=False).astype(jnp.bfloat16)
        pairs = [(i, (i + shift) % size) for i in range(size)]
        total = total + lax.ppermute(sent, name, pairs).astype(jnp.float32)
    return total


def reduce_rows(attended, out_weight):
    x_size, zl_size, c_size = [lax.axis_size(name) for name in HEAD]
    rows, width = attended.shape
    share = rows // (x_size * zl_size * c_size)
    order = attended.reshape(x_size, zl_size, c_size, share, width).transpose(2, 0, 1, 3, 4)
    columns = out_weight.shape[1]
    me = lax.axis_index("c")
    total = None
    for shift in range(c_size):
        rows_for = lax.dynamic_index_in_dim(order, (me + shift) % c_size, 0, keepdims=False)
        piece = jnp.dot(rows_for.reshape(-1, width), out_weight, preferred_element_type=jnp.float32)
        piece = piece.astype(jnp.bfloat16).reshape(x_size, zl_size, share, columns)
        if shift:
            pairs = [(i, (i + shift) % c_size) for i in range(c_size)]
            total = total + lax.ppermute(piece, "c", pairs).astype(jnp.float32)
        else:
            total = piece.astype(jnp.float32)
    total = exchange(total.reshape(x_size, zl_size, share, columns), "x")
    total = exchange(total.reshape(zl_size, share, columns), "zl")
    return total.astype(jnp.bfloat16)


def solution(mesh):
    seq_size, head_size = mesh.shape["seq"], mesh.shape["head"]
    fine = Mesh(mesh.devices.reshape(seq_size // 4, 4, head_size // 4, 2, 2), SEQ + HEAD)
    placed = (
        P(SEQ, HEAD),
        P(SEQ, HEAD),
        P(SEQ, HEAD),
        P(),
        P(),
        P(HEAD, None),
        P(None, SEQ, HEAD),
        P(None, SEQ, HEAD),
        P(),
    )
    return jax.shard_map(
        local,
        mesh=fine,
        in_specs=placed,
        out_specs=(
            P(SEQ, HEAD),
            P(SEQ + HEAD, None),
            P(None, SEQ, None, HEAD),
            P(None, SEQ, None, HEAD),
        ),
        check_vma=False,
    )
```

```python
import functools
import math

import jax
import jax.numpy as jnp
from jax import lax
from jax.experimental import pallas as pl
from jax.experimental.pallas import tpu as pltpu
from jax.sharding import Mesh
from jax.sharding import PartitionSpec as P

HD = 128
SEQ = ("zh", "y")
HEAD = ("x", "zl", "c")
Q_ROWS = 512


def relayout(cache_keys, cache_values, page_table):
    position = lax.axis_index(SEQ)
    groups = lax.axis_size(SEQ)
    layers, block_rows, feat_width = cache_keys.shape
    page_count = page_table.shape[0] // groups
    page_len = block_rows // page_count
    per_group = page_count // groups
    table = page_table.reshape(groups, groups, per_group)
    own = lax.dynamic_index_in_dim(table, position, 0, keepdims=False)
    run_ids = jnp.arange(groups, dtype=jnp.int32)
    goes = (own[:, 0] // page_count)[None, :] == run_ids[:, None]
    run_of = jnp.sum(jnp.where(goes, run_ids[None, :], 0), axis=1)
    send_pages = (run_of[:, None] * per_group + jnp.arange(per_group, dtype=jnp.int32)[None, :]).reshape(-1)
    both = jnp.stack([cache_keys, cache_values]).reshape(2, layers, page_count, page_len, feat_width)
    outgoing = jnp.take(both, send_pages, axis=2).reshape(2, layers, groups, per_group, page_len, feat_width)
    outgoing = outgoing.transpose(2, 0, 1, 3, 4, 5)
    hit = (table[:, :, 0] // page_count) == position
    slot_of = (jnp.sum(jnp.where(hit[:, :, None], table, 0), axis=1) % page_count).reshape(-1)
    arrivals = jnp.arange(page_count, dtype=jnp.int32)
    inverse = jnp.sum(jnp.where(slot_of[None, :] == arrivals[:, None], arrivals[None, :], 0), axis=1)
    return (outgoing, inverse)


def place_pages(outgoing, inverse):
    moved = lax.all_to_all(outgoing, SEQ, split_axis=0, concat_axis=0, tiled=True)
    per_group = moved.shape[3]
    source, page = inverse // per_group, inverse % per_group
    return tuple(moved[source, kind, :, page].transpose(1, 0, 2, 3) for kind in range(moved.shape[1]))


def attention_kernel(meta_ref, q_ref, qseg_ref, kseg_ref, k_ref, v_ref, o_ref, *, block_count, scale):
    chunk = pl.program_id(1)
    query_block = meta_ref[block_count]
    q = q_ref[...]
    qseg = qseg_ref[...]
    rows = q.shape[0]
    block_rows = k_ref.shape[1]
    local_pos = chunk * rows + lax.broadcasted_iota(jnp.int32, (rows, 1), 0)
    key_pos = lax.broadcasted_iota(jnp.int32, (1, block_rows), 1)

    def step(c, carry, allowed):
        row_best, weight_sum, numerator = carry
        s = lax.dot_general(q, k_ref[c], (((1,), (1,)), ((), ())), preferred_element_type=jnp.float32) * scale
        if allowed is not None:
            s = jnp.where(allowed, s, -jnp.inf)
        new_best = jnp.maximum(row_best, jnp.max(s, axis=1, keepdims=True))
        rescale = jnp.exp(row_best - new_best)
        w = jnp.exp(s - new_best)
        weight_sum = rescale * weight_sum + jnp.sum(w, axis=1, keepdims=True)
        added = jnp.dot(w.astype(jnp.bfloat16), v_ref[c], preferred_element_type=jnp.float32)
        return (new_best, weight_sum, rescale * numerator + added)

    initial = (
        jnp.full((rows, 1), -jnp.inf, jnp.float32),
        jnp.zeros((rows, 1), jnp.float32),
        jnp.zeros((rows, q.shape[1]), jnp.float32),
    )
    carry = step(query_block, initial, (qseg == kseg_ref[query_block]) & (key_pos <= local_pos))

    def body(c, carry):
        flag = meta_ref[c]
        return lax.cond(
            flag == 0,
            lambda x: x,
            lambda x: lax.cond(
                flag == 1,
                lambda y: step(c, y, qseg == kseg_ref[c]),
                lambda y: step(c, y, None),
                x,
            ),
            carry,
        )

    _, weight_sum, numerator = lax.fori_loop(0, query_block, body, carry)
    o_ref[...] = (numerator / weight_sum).astype(o_ref.dtype)


def attend(meta, queries, qseg, kseg, kv):
    block_count, _, block_rows, _ = kv.shape
    rows, feat_width = queries.shape
    kernel = functools.partial(attention_kernel, block_count=block_count, scale=1.0 / math.sqrt(HD))
    return pl.pallas_call(
        kernel,
        grid_spec=pltpu.PrefetchScalarGridSpec(
            num_scalar_prefetch=1,
            grid=(feat_width // HD, rows // Q_ROWS),
            in_specs=[
                pl.BlockSpec((Q_ROWS, HD), lambda h, i, meta: (i, h)),
                pl.BlockSpec((Q_ROWS, 1), lambda h, i, meta: (i, 0)),
                pl.BlockSpec((block_count, 1, block_rows), lambda h, i, meta: (0, 0, 0)),
                pl.BlockSpec((block_count, None, block_rows, HD), lambda h, i, meta: (0, 0, 0, h)),
                pl.BlockSpec((block_count, None, block_rows, HD), lambda h, i, meta: (0, 1, 0, h)),
            ],
            out_specs=pl.BlockSpec((Q_ROWS, HD), lambda h, i, meta: (i, h)),
        ),
        out_shape=jax.ShapeDtypeStruct((rows, feat_width), queries.dtype),
    )(meta, queries, qseg, kseg, kv, kv)


def attention(queries, stretch_keys, stretch_values, segment_ids, block_live, moved):
    position = lax.axis_index(SEQ)
    block_count = lax.axis_size(SEQ)
    block_rows, feat_width = queries.shape
    head_count = feat_width // HD
    seg_blocks = segment_ids.reshape(block_count, block_rows)
    query_seg = lax.dynamic_index_in_dim(seg_blocks, position, 0, keepdims=False)
    live_row = lax.dynamic_index_in_dim(block_live, position, 0, keepdims=False)
    block_ids = jnp.arange(block_count, dtype=jnp.int32)
    earlier = (block_ids < position) & (live_row == 1) & (seg_blocks[:, -1] >= query_seg[0])
    whole = earlier & (seg_blocks[:, 0] == query_seg[-1])
    flags = jnp.where(whole, 2, jnp.where(earlier, 1, 0)).astype(jnp.int32)
    meta = jnp.concatenate([flags, position.astype(jnp.int32)[None]])
    qseg = query_seg[:, None]
    kseg = seg_blocks[:, None, :]
    kv = jnp.stack([stretch_keys, stretch_values])
    kv_all = lax.all_gather(kv, SEQ, axis=0, tiled=False)
    moved, kv_all = lax.optimization_barrier((moved, kv_all))
    return (attend(meta, queries, qseg, kseg, kv_all), moved)


def local(
    queries,
    stretch_keys,
    stretch_values,
    segment_ids,
    block_live,
    out_weight,
    cache_keys,
    cache_values,
    page_table,
):
    moved, inverse = relayout(cache_keys, cache_values, page_table)
    attended, moved = attention(queries, stretch_keys, stretch_values, segment_ids, block_live, moved)
    decode_keys, decode_values = place_pages(moved, inverse)
    projected = reduce_rows(attended, out_weight)
    return (attended, projected, decode_keys, decode_values)


def exchange(pieces, name):
    size = pieces.shape[0]
    me = lax.axis_index(name)
    total = lax.dynamic_index_in_dim(pieces, me, 0, keepdims=False).astype(jnp.float32)
    for shift in range(1, size):
        target = (me + shift) % size
        sent = lax.dynamic_index_in_dim(pieces, target, 0, keepdims=False).astype(jnp.bfloat16)
        pairs = [(i, (i + shift) % size) for i in range(size)]
        total = total + lax.ppermute(sent, name, pairs).astype(jnp.float32)
    return total


def reduce_rows(attended, out_weight):
    x_size, zl_size, c_size = [lax.axis_size(name) for name in HEAD]
    rows, width = attended.shape
    share = rows // (x_size * zl_size * c_size)
    order = attended.reshape(x_size, zl_size, c_size, share, width).transpose(2, 0, 1, 3, 4)
    columns = out_weight.shape[1]
    me = lax.axis_index("c")
    total = None
    for shift in range(c_size):
        rows_for = lax.dynamic_index_in_dim(order, (me + shift) % c_size, 0, keepdims=False)
        piece = jnp.dot(rows_for.reshape(-1, width), out_weight, preferred_element_type=jnp.float32)
        piece = piece.astype(jnp.bfloat16).reshape(x_size, zl_size, share, columns)
        if shift:
            pairs = [(i, (i + shift) % c_size) for i in range(c_size)]
            total = total + lax.ppermute(piece, "c", pairs).astype(jnp.float32)
        else:
            total = piece.astype(jnp.float32)
    total = exchange(total.reshape(x_size, zl_size, share, columns), "x")
    total = exchange(total.reshape(zl_size, share, columns), "zl")
    return total.astype(jnp.bfloat16)


def solution(mesh):
    seq_size, head_size = mesh.shape["seq"], mesh.shape["head"]
    fine = Mesh(mesh.devices.reshape(seq_size // 4, 4, head_size // 4, 2, 2), SEQ + HEAD)
    placed = (
        P(SEQ, HEAD),
        P(SEQ, HEAD),
        P(SEQ, HEAD),
        P(),
        P(),
        P(HEAD, None),
        P(None, SEQ, HEAD),
        P(None, SEQ, HEAD),
        P(),
    )
    return jax.shard_map(
        local,
        mesh=fine,
        in_specs=placed,
        out_specs=(
            P(SEQ, HEAD),
            P(SEQ + HEAD, None),
            P(None, SEQ, None, HEAD),
            P(None, SEQ, None, HEAD),
        ),
        check_vma=False,
    )
```

```python
import functools
import math

import jax
import jax.numpy as jnp
from jax import lax
from jax.experimental import pallas as pl
from jax.experimental.pallas import tpu as pltpu
from jax.sharding import Mesh
from jax.sharding import PartitionSpec as P

HD = 128
SEQ = ("zh", "y")
HEAD = ("x", "zl", "c")
Q_ROWS = 512


def relayout(cache_keys, cache_values, page_table):
    position = lax.axis_index(SEQ)
    groups = lax.axis_size(SEQ)
    layers, block_rows, feat_width = cache_keys.shape
    page_count = page_table.shape[0] // groups
    page_len = block_rows // page_count
    per_group = page_count // groups
    table = page_table.reshape(groups, groups, per_group)
    own = lax.dynamic_index_in_dim(table, position, 0, keepdims=False)
    run_ids = jnp.arange(groups, dtype=jnp.int32)
    goes = (own[:, 0] // page_count)[None, :] == run_ids[:, None]
    run_of = jnp.sum(jnp.where(goes, run_ids[None, :], 0), axis=1)
    send_pages = (run_of[:, None] * per_group + jnp.arange(per_group, dtype=jnp.int32)[None, :]).reshape(-1)
    both = jnp.stack([cache_keys, cache_values]).reshape(2, layers, page_count, page_len, feat_width)
    outgoing = jnp.take(both, send_pages, axis=2).reshape(2, layers, groups, per_group, page_len, feat_width)
    outgoing = outgoing.transpose(2, 0, 1, 3, 4, 5)
    hit = (table[:, :, 0] // page_count) == position
    slot_of = (jnp.sum(jnp.where(hit[:, :, None], table, 0), axis=1) % page_count).reshape(-1)
    arrivals = jnp.arange(page_count, dtype=jnp.int32)
    inverse = jnp.sum(jnp.where(slot_of[None, :] == arrivals[:, None], arrivals[None, :], 0), axis=1)
    return (outgoing, inverse)


def place_pages(moved, inverse):
    _, kinds, layers, per_group, page_len, feat_width = moved.shape
    moved = moved.transpose(1, 2, 0, 3, 4, 5).reshape(kinds, layers, -1, page_len, feat_width)
    placed = jnp.take(moved, inverse, axis=2)
    return (placed[0], placed[1])


def attention_kernel(meta_ref, q_ref, qseg_ref, kseg_ref, k_ref, v_ref, o_ref, *, block_count, scale):
    chunk = pl.program_id(1)
    query_block = meta_ref[block_count]
    q = q_ref[...]
    qseg = qseg_ref[...]
    rows = q.shape[0]
    block_rows = k_ref.shape[1]
    local_pos = chunk * rows + lax.broadcasted_iota(jnp.int32, (rows, 1), 0)
    key_pos = lax.broadcasted_iota(jnp.int32, (1, block_rows), 1)

    def step(c, carry, allowed):
        row_best, weight_sum, numerator = carry
        s = lax.dot_general(q, k_ref[c], (((1,), (1,)), ((), ())), preferred_element_type=jnp.float32) * scale
        if allowed is not None:
            s = jnp.where(allowed, s, -jnp.inf)
        new_best = jnp.maximum(row_best, jnp.max(s, axis=1, keepdims=True))
        rescale = jnp.exp(row_best - new_best)
        w = jnp.exp(s - new_best)
        weight_sum = rescale * weight_sum + jnp.sum(w, axis=1, keepdims=True)
        added = jnp.dot(w.astype(jnp.bfloat16), v_ref[c], preferred_element_type=jnp.float32)
        return (new_best, weight_sum, rescale * numerator + added)

    initial = (
        jnp.full((rows, 1), -jnp.inf, jnp.float32),
        jnp.zeros((rows, 1), jnp.float32),
        jnp.zeros((rows, q.shape[1]), jnp.float32),
    )
    carry = step(query_block, initial, (qseg == kseg_ref[query_block]) & (key_pos <= local_pos))

    def body(c, carry):
        flag = meta_ref[c]
        return lax.cond(
            flag == 0,
            lambda x: x,
            lambda x: lax.cond(
                flag == 1,
                lambda y: step(c, y, qseg == kseg_ref[c]),
                lambda y: step(c, y, None),
                x,
            ),
            carry,
        )

    _, weight_sum, numerator = lax.fori_loop(0, query_block, body, carry)
    o_ref[...] = (numerator / weight_sum).astype(o_ref.dtype)


def attend(meta, queries, qseg, kseg, kv):
    block_count, _, block_rows, _ = kv.shape
    rows, feat_width = queries.shape
    kernel = functools.partial(attention_kernel, block_count=block_count, scale=1.0 / math.sqrt(HD))
    return pl.pallas_call(
        kernel,
        grid_spec=pltpu.PrefetchScalarGridSpec(
            num_scalar_prefetch=1,
            grid=(feat_width // HD, rows // Q_ROWS),
            in_specs=[
                pl.BlockSpec((Q_ROWS, HD), lambda h, i, meta: (i, h)),
                pl.BlockSpec((Q_ROWS, 1), lambda h, i, meta: (i, 0)),
                pl.BlockSpec((block_count, 1, block_rows), lambda h, i, meta: (0, 0, 0)),
                pl.BlockSpec((block_count, None, block_rows, HD), lambda h, i, meta: (0, 0, 0, h)),
                pl.BlockSpec((block_count, None, block_rows, HD), lambda h, i, meta: (0, 1, 0, h)),
            ],
            out_specs=pl.BlockSpec((Q_ROWS, HD), lambda h, i, meta: (i, h)),
        ),
        out_shape=jax.ShapeDtypeStruct((rows, feat_width), queries.dtype),
    )(meta, queries, qseg, kseg, kv, kv)


def attention(queries, stretch_keys, stretch_values, segment_ids, block_live, moved):
    position = lax.axis_index(SEQ)
    block_count = lax.axis_size(SEQ)
    block_rows, feat_width = queries.shape
    head_count = feat_width // HD
    seg_blocks = segment_ids.reshape(block_count, block_rows)
    query_seg = lax.dynamic_index_in_dim(seg_blocks, position, 0, keepdims=False)
    live_row = lax.dynamic_index_in_dim(block_live, position, 0, keepdims=False)
    block_ids = jnp.arange(block_count, dtype=jnp.int32)
    earlier = (block_ids < position) & (live_row == 1) & (seg_blocks[:, -1] >= query_seg[0])
    whole = earlier & (seg_blocks[:, 0] == query_seg[-1])
    flags = jnp.where(whole, 2, jnp.where(earlier, 1, 0)).astype(jnp.int32)
    meta = jnp.concatenate([flags, position.astype(jnp.int32)[None]])
    qseg = query_seg[:, None]
    kseg = seg_blocks[:, None, :]
    kv = jnp.stack([stretch_keys, stretch_values])
    kv_all = lax.all_gather(kv, SEQ, axis=0, tiled=False)
    moved, kv_all = lax.optimization_barrier((moved, kv_all))
    return (attend(meta, queries, qseg, kseg, kv_all), moved)


def local(
    queries,
    stretch_keys,
    stretch_values,
    segment_ids,
    block_live,
    out_weight,
    cache_keys,
    cache_values,
    page_table,
):
    moved, inverse = relayout(cache_keys, cache_values, page_table)
    attended, moved = attention(queries, stretch_keys, stretch_values, segment_ids, block_live, moved)
    moved = lax.all_to_all(moved, SEQ, split_axis=0, concat_axis=0, tiled=True)
    projected, moved = reduce_rows(attended, out_weight, moved)
    decode_keys, decode_values = place_pages(moved, inverse)
    return (attended, projected, decode_keys, decode_values)


def exchange(pieces, name):
    size = pieces.shape[0]
    me = lax.axis_index(name)
    total = lax.dynamic_index_in_dim(pieces, me, 0, keepdims=False).astype(jnp.float32)
    for shift in range(1, size):
        target = (me + shift) % size
        sent = lax.dynamic_index_in_dim(pieces, target, 0, keepdims=False).astype(jnp.bfloat16)
        pairs = [(i, (i + shift) % size) for i in range(size)]
        total = total + lax.ppermute(sent, name, pairs).astype(jnp.float32)
    return total


def reduce_rows(attended, out_weight, moved):
    x_size, zl_size, c_size = [lax.axis_size(name) for name in HEAD]
    rows, width = attended.shape
    share = rows // (x_size * zl_size * c_size)
    order = attended.reshape(x_size, zl_size, c_size, share, width).transpose(2, 0, 1, 3, 4)
    columns = out_weight.shape[1]
    me = lax.axis_index("c")
    total = None
    for shift in range(c_size):
        rows_for = lax.dynamic_index_in_dim(order, (me + shift) % c_size, 0, keepdims=False)
        piece = jnp.dot(rows_for.reshape(-1, width), out_weight, preferred_element_type=jnp.float32)
        piece = piece.astype(jnp.bfloat16).reshape(x_size, zl_size, share, columns)
        if shift:
            pairs = [(i, (i + shift) % c_size) for i in range(c_size)]
            total = total + lax.ppermute(piece, "c", pairs).astype(jnp.float32)
        else:
            total = piece.astype(jnp.float32)
    total = exchange(total.reshape(x_size, zl_size, share, columns), "x")
    total, moved = lax.optimization_barrier((total, moved))
    total = exchange(total.reshape(zl_size, share, columns), "zl")
    return (total.astype(jnp.bfloat16), moved)


def solution(mesh):
    seq_size, head_size = mesh.shape["seq"], mesh.shape["head"]
    fine = Mesh(mesh.devices.reshape(seq_size // 4, 4, head_size // 4, 2, 2), SEQ + HEAD)
    placed = (
        P(SEQ, HEAD),
        P(SEQ, HEAD),
        P(SEQ, HEAD),
        P(),
        P(),
        P(HEAD, None),
        P(None, SEQ, HEAD),
        P(None, SEQ, HEAD),
        P(),
    )
    return jax.shard_map(
        local,
        mesh=fine,
        in_specs=placed,
        out_specs=(
            P(SEQ, HEAD),
            P(SEQ + HEAD, None),
            P(None, SEQ, None, HEAD),
            P(None, SEQ, None, HEAD),
        ),
        check_vma=False,
    )
```

```python
import functools
import math

import jax
import jax.numpy as jnp
from jax import lax
from jax.experimental import pallas as pl
from jax.experimental.pallas import tpu as pltpu
from jax.sharding import Mesh
from jax.sharding import PartitionSpec as P

HD = 128
SEQ = ("zh", "y")
HEAD = ("x", "zl", "c")
Q_ROWS = 512


def relayout(cache_keys, cache_values, page_table):
    position = lax.axis_index(SEQ)
    groups = lax.axis_size(SEQ)
    layers, block_rows, feat_width = cache_keys.shape
    page_count = page_table.shape[0] // groups
    page_len = block_rows // page_count
    per_group = page_count // groups
    table = page_table.reshape(groups, groups, per_group)
    own = lax.dynamic_index_in_dim(table, position, 0, keepdims=False)
    run_ids = jnp.arange(groups, dtype=jnp.int32)
    goes = (own[:, 0] // page_count)[None, :] == run_ids[:, None]
    run_of = jnp.sum(jnp.where(goes, run_ids[None, :], 0), axis=1)
    send_pages = (run_of[:, None] * per_group + jnp.arange(per_group, dtype=jnp.int32)[None, :]).reshape(-1)
    both = jnp.stack([cache_keys, cache_values]).reshape(2, layers, page_count, page_len, feat_width)
    outgoing = jnp.take(both, send_pages, axis=2).reshape(2, layers, groups, per_group, page_len, feat_width)
    outgoing = outgoing.transpose(2, 0, 1, 3, 4, 5)
    hit = (table[:, :, 0] // page_count) == position
    slot_of = (jnp.sum(jnp.where(hit[:, :, None], table, 0), axis=1) % page_count).reshape(-1)
    arrivals = jnp.arange(page_count, dtype=jnp.int32)
    inverse = jnp.sum(jnp.where(slot_of[None, :] == arrivals[:, None], arrivals[None, :], 0), axis=1)
    return (outgoing, inverse)


def place_pages(outgoing, inverse):
    moved = lax.all_to_all(outgoing, SEQ[0], split_axis=0, concat_axis=0, tiled=True)
    moved = moved.reshape(-1, *moved.shape[2:])
    _, kinds, layers, per_group, page_len, feat_width = moved.shape
    moved = moved.transpose(1, 2, 0, 3, 4, 5).reshape(kinds, layers, -1, page_len, feat_width)
    placed = jnp.take(moved, inverse, axis=2)
    return (placed[0], placed[1])


def attention_kernel(meta_ref, q_ref, qseg_ref, kseg_ref, k_ref, v_ref, o_ref, *, block_count, scale):
    chunk = pl.program_id(1)
    query_block = meta_ref[block_count]
    q = q_ref[...]
    qseg = qseg_ref[...]
    rows = q.shape[0]
    block_rows = k_ref.shape[1]
    local_pos = chunk * rows + lax.broadcasted_iota(jnp.int32, (rows, 1), 0)
    key_pos = lax.broadcasted_iota(jnp.int32, (1, block_rows), 1)

    def step(c, carry, allowed):
        row_best, weight_sum, numerator = carry
        s = lax.dot_general(q, k_ref[c], (((1,), (1,)), ((), ())), preferred_element_type=jnp.float32) * scale
        if allowed is not None:
            s = jnp.where(allowed, s, -jnp.inf)
        new_best = jnp.maximum(row_best, jnp.max(s, axis=1, keepdims=True))
        rescale = jnp.exp(row_best - new_best)
        w = jnp.exp(s - new_best)
        weight_sum = rescale * weight_sum + jnp.sum(w, axis=1, keepdims=True)
        added = jnp.dot(w.astype(jnp.bfloat16), v_ref[c], preferred_element_type=jnp.float32)
        return (new_best, weight_sum, rescale * numerator + added)

    initial = (
        jnp.full((rows, 1), -jnp.inf, jnp.float32),
        jnp.zeros((rows, 1), jnp.float32),
        jnp.zeros((rows, q.shape[1]), jnp.float32),
    )
    carry = step(query_block, initial, (qseg == kseg_ref[query_block]) & (key_pos <= local_pos))

    def body(c, carry):
        flag = meta_ref[c]
        return lax.cond(
            flag == 0,
            lambda x: x,
            lambda x: lax.cond(
                flag == 1,
                lambda y: step(c, y, qseg == kseg_ref[c]),
                lambda y: step(c, y, None),
                x,
            ),
            carry,
        )

    _, weight_sum, numerator = lax.fori_loop(0, query_block, body, carry)
    o_ref[...] = (numerator / weight_sum).astype(o_ref.dtype)


def attend(meta, queries, qseg, kseg, kv):
    block_count, _, block_rows, _ = kv.shape
    rows, feat_width = queries.shape
    kernel = functools.partial(attention_kernel, block_count=block_count, scale=1.0 / math.sqrt(HD))
    return pl.pallas_call(
        kernel,
        grid_spec=pltpu.PrefetchScalarGridSpec(
            num_scalar_prefetch=1,
            grid=(feat_width // HD, rows // Q_ROWS),
            in_specs=[
                pl.BlockSpec((Q_ROWS, HD), lambda h, i, meta: (i, h)),
                pl.BlockSpec((Q_ROWS, 1), lambda h, i, meta: (i, 0)),
                pl.BlockSpec((block_count, 1, block_rows), lambda h, i, meta: (0, 0, 0)),
                pl.BlockSpec((block_count, None, block_rows, HD), lambda h, i, meta: (0, 0, 0, h)),
                pl.BlockSpec((block_count, None, block_rows, HD), lambda h, i, meta: (0, 1, 0, h)),
            ],
            out_specs=pl.BlockSpec((Q_ROWS, HD), lambda h, i, meta: (i, h)),
        ),
        out_shape=jax.ShapeDtypeStruct((rows, feat_width), queries.dtype),
    )(meta, queries, qseg, kseg, kv, kv)


def attention(queries, stretch_keys, stretch_values, segment_ids, block_live, moved):
    position = lax.axis_index(SEQ)
    block_count = lax.axis_size(SEQ)
    block_rows, feat_width = queries.shape
    head_count = feat_width // HD
    seg_blocks = segment_ids.reshape(block_count, block_rows)
    query_seg = lax.dynamic_index_in_dim(seg_blocks, position, 0, keepdims=False)
    live_row = lax.dynamic_index_in_dim(block_live, position, 0, keepdims=False)
    block_ids = jnp.arange(block_count, dtype=jnp.int32)
    earlier = (block_ids < position) & (live_row == 1) & (seg_blocks[:, -1] >= query_seg[0])
    whole = earlier & (seg_blocks[:, 0] == query_seg[-1])
    flags = jnp.where(whole, 2, jnp.where(earlier, 1, 0)).astype(jnp.int32)
    meta = jnp.concatenate([flags, position.astype(jnp.int32)[None]])
    qseg = query_seg[:, None]
    kseg = seg_blocks[:, None, :]
    kv = jnp.stack([stretch_keys, stretch_values])
    kv_all = lax.all_gather(kv, SEQ, axis=0, tiled=False)
    planes = lax.axis_size(SEQ[0])
    moved = moved.reshape(planes, -1, *moved.shape[1:])
    moved = lax.all_to_all(moved, SEQ[1], split_axis=1, concat_axis=1, tiled=True)
    moved, kv_all = lax.optimization_barrier((moved, kv_all))
    return (attend(meta, queries, qseg, kseg, kv_all), moved)


def local(
    queries,
    stretch_keys,
    stretch_values,
    segment_ids,
    block_live,
    out_weight,
    cache_keys,
    cache_values,
    page_table,
):
    moved, inverse = relayout(cache_keys, cache_values, page_table)
    attended, moved = attention(queries, stretch_keys, stretch_values, segment_ids, block_live, moved)
    decode_keys, decode_values = place_pages(moved, inverse)
    projected = reduce_rows(attended, out_weight)
    return (attended, projected, decode_keys, decode_values)


def exchange(pieces, name):
    size = pieces.shape[0]
    me = lax.axis_index(name)
    total = lax.dynamic_index_in_dim(pieces, me, 0, keepdims=False).astype(jnp.float32)
    for shift in range(1, size):
        target = (me + shift) % size
        sent = lax.dynamic_index_in_dim(pieces, target, 0, keepdims=False).astype(jnp.bfloat16)
        pairs = [(i, (i + shift) % size) for i in range(size)]
        total = total + lax.ppermute(sent, name, pairs).astype(jnp.float32)
    return total


def reduce_rows(attended, out_weight):
    x_size, zl_size, c_size = [lax.axis_size(name) for name in HEAD]
    rows, width = attended.shape
    share = rows // (x_size * zl_size * c_size)
    order = attended.reshape(x_size, zl_size, c_size, share, width).transpose(2, 0, 1, 3, 4)
    columns = out_weight.shape[1]
    me = lax.axis_index("c")
    total = None
    for shift in range(c_size):
        rows_for = lax.dynamic_index_in_dim(order, (me + shift) % c_size, 0, keepdims=False)
        piece = jnp.dot(rows_for.reshape(-1, width), out_weight, preferred_element_type=jnp.float32)
        piece = piece.astype(jnp.bfloat16).reshape(x_size, zl_size, share, columns)
        if shift:
            pairs = [(i, (i + shift) % c_size) for i in range(c_size)]
            total = total + lax.ppermute(piece, "c", pairs).astype(jnp.float32)
        else:
            total = piece.astype(jnp.float32)
    total = exchange(total.reshape(x_size, zl_size, share, columns), "x")
    total = exchange(total.reshape(zl_size, share, columns), "zl")
    return total.astype(jnp.bfloat16)


def solution(mesh):
    seq_size, head_size = mesh.shape["seq"], mesh.shape["head"]
    fine = Mesh(mesh.devices.reshape(seq_size // 4, 4, head_size // 4, 2, 2), SEQ + HEAD)
    placed = (
        P(SEQ, HEAD),
        P(SEQ, HEAD),
        P(SEQ, HEAD),
        P(),
        P(),
        P(HEAD, None),
        P(None, SEQ, HEAD),
        P(None, SEQ, HEAD),
        P(),
    )
    return jax.shard_map(
        local,
        mesh=fine,
        in_specs=placed,
        out_specs=(
            P(SEQ, HEAD),
            P(SEQ + HEAD, None),
            P(None, SEQ, None, HEAD),
            P(None, SEQ, None, HEAD),
        ),
        check_vma=False,
    )
```

```python
import functools
import math

import jax
import jax.numpy as jnp
from jax import lax
from jax.experimental import pallas as pl
from jax.experimental.pallas import tpu as pltpu
from jax.sharding import Mesh
from jax.sharding import PartitionSpec as P

HD = 128
SEQ = ("zh", "y")
HEAD = ("x", "zl", "c")
Q_ROWS = 512


def relayout(cache_keys, cache_values, page_table):
    position = lax.axis_index(SEQ)
    groups = lax.axis_size(SEQ)
    layers, block_rows, feat_width = cache_keys.shape
    page_count = page_table.shape[0] // groups
    page_len = block_rows // page_count
    per_group = page_count // groups
    table = page_table.reshape(groups, groups, per_group)
    own = lax.dynamic_index_in_dim(table, position, 0, keepdims=False)
    run_ids = jnp.arange(groups, dtype=jnp.int32)
    goes = (own[:, 0] // page_count)[None, :] == run_ids[:, None]
    run_of = jnp.sum(jnp.where(goes, run_ids[None, :], 0), axis=1)
    send_pages = (run_of[:, None] * per_group + jnp.arange(per_group, dtype=jnp.int32)[None, :]).reshape(-1)
    both = jnp.stack([cache_keys, cache_values]).reshape(2, layers, page_count, page_len, feat_width)
    outgoing = jnp.take(both, send_pages, axis=2).reshape(2, layers, groups, per_group, page_len, feat_width)
    outgoing = outgoing.transpose(2, 0, 1, 3, 4, 5)
    hit = (table[:, :, 0] // page_count) == position
    slot_of = (jnp.sum(jnp.where(hit[:, :, None], table, 0), axis=1) % page_count).reshape(-1)
    arrivals = jnp.arange(page_count, dtype=jnp.int32)
    inverse = jnp.sum(jnp.where(slot_of[None, :] == arrivals[:, None], arrivals[None, :], 0), axis=1)
    return (outgoing, inverse)


def place_pages(outgoing, inverse):
    moved = lax.all_to_all(outgoing, SEQ, split_axis=0, concat_axis=0, tiled=True)
    _, kinds, layers, per_group, page_len, feat_width = moved.shape
    moved = moved.transpose(1, 2, 0, 3, 4, 5).reshape(kinds, layers, -1, page_len, feat_width)
    placed = jnp.take(moved, inverse, axis=2)
    return (placed[0], placed[1])


def attention_kernel(meta_ref, q_ref, qseg_ref, kseg_ref, k_ref, v_ref, o_ref, *, block_count, scale):
    chunk = pl.program_id(1)
    query_block = meta_ref[block_count]
    q = q_ref[...]
    qseg = qseg_ref[...]
    rows = q.shape[0]
    block_rows = k_ref.shape[1]
    local_pos = chunk * rows + lax.broadcasted_iota(jnp.int32, (rows, 1), 0)
    key_pos = lax.broadcasted_iota(jnp.int32, (1, block_rows), 1)

    def step(c, carry, allowed):
        row_best, weight_sum, numerator = carry
        s = lax.dot_general(q, k_ref[c], (((1,), (1,)), ((), ())), preferred_element_type=jnp.float32) * scale
        if allowed is not None:
            s = jnp.where(allowed, s, -jnp.inf)
        new_best = jnp.maximum(row_best, jnp.max(s, axis=1, keepdims=True))
        rescale = jnp.exp(row_best - new_best)
        w = jnp.exp(s - new_best).astype(jnp.bfloat16)
        sums = jnp.dot(w, jnp.ones((block_rows, numerator.shape[1]), jnp.bfloat16), preferred_element_type=jnp.float32)
        added = jnp.dot(w, v_ref[c], preferred_element_type=jnp.float32)
        return (new_best, rescale * weight_sum + sums, rescale * numerator + added)

    initial = (
        jnp.full((rows, 1), -jnp.inf, jnp.float32),
        jnp.zeros((rows, q.shape[1]), jnp.float32),
        jnp.zeros((rows, q.shape[1]), jnp.float32),
    )
    carry = step(query_block, initial, (qseg == kseg_ref[query_block]) & (key_pos <= local_pos))

    def body(c, carry):
        flag = meta_ref[c]
        return lax.cond(
            flag == 0,
            lambda x: x,
            lambda x: lax.cond(
                flag == 1,
                lambda y: step(c, y, qseg == kseg_ref[c]),
                lambda y: step(c, y, None),
                x,
            ),
            carry,
        )

    _, weight_sum, numerator = lax.fori_loop(0, query_block, body, carry)
    o_ref[...] = (numerator / weight_sum).astype(o_ref.dtype)


def attend(meta, queries, qseg, kseg, kv):
    block_count, _, block_rows, _ = kv.shape
    rows, feat_width = queries.shape
    kernel = functools.partial(attention_kernel, block_count=block_count, scale=1.0 / math.sqrt(HD))
    return pl.pallas_call(
        kernel,
        grid_spec=pltpu.PrefetchScalarGridSpec(
            num_scalar_prefetch=1,
            grid=(feat_width // HD, rows // Q_ROWS),
            in_specs=[
                pl.BlockSpec((Q_ROWS, HD), lambda h, i, meta: (i, h)),
                pl.BlockSpec((Q_ROWS, 1), lambda h, i, meta: (i, 0)),
                pl.BlockSpec((block_count, 1, block_rows), lambda h, i, meta: (0, 0, 0)),
                pl.BlockSpec((block_count, None, block_rows, HD), lambda h, i, meta: (0, 0, 0, h)),
                pl.BlockSpec((block_count, None, block_rows, HD), lambda h, i, meta: (0, 1, 0, h)),
            ],
            out_specs=pl.BlockSpec((Q_ROWS, HD), lambda h, i, meta: (i, h)),
        ),
        out_shape=jax.ShapeDtypeStruct((rows, feat_width), queries.dtype),
    )(meta, queries, qseg, kseg, kv, kv)


def attention(queries, stretch_keys, stretch_values, segment_ids, block_live, moved):
    position = lax.axis_index(SEQ)
    block_count = lax.axis_size(SEQ)
    block_rows, feat_width = queries.shape
    head_count = feat_width // HD
    seg_blocks = segment_ids.reshape(block_count, block_rows)
    query_seg = lax.dynamic_index_in_dim(seg_blocks, position, 0, keepdims=False)
    live_row = lax.dynamic_index_in_dim(block_live, position, 0, keepdims=False)
    block_ids = jnp.arange(block_count, dtype=jnp.int32)
    earlier = (block_ids < position) & (live_row == 1) & (seg_blocks[:, -1] >= query_seg[0])
    whole = earlier & (seg_blocks[:, 0] == query_seg[-1])
    flags = jnp.where(whole, 2, jnp.where(earlier, 1, 0)).astype(jnp.int32)
    meta = jnp.concatenate([flags, position.astype(jnp.int32)[None]])
    qseg = query_seg[:, None]
    kseg = seg_blocks[:, None, :]
    kv = jnp.stack([stretch_keys, stretch_values])
    kv_all = lax.all_gather(kv, SEQ, axis=0, tiled=False)
    moved, kv_all = lax.optimization_barrier((moved, kv_all))
    return (attend(meta, queries, qseg, kseg, kv_all), moved)


def local(
    queries,
    stretch_keys,
    stretch_values,
    segment_ids,
    block_live,
    out_weight,
    cache_keys,
    cache_values,
    page_table,
):
    moved, inverse = relayout(cache_keys, cache_values, page_table)
    attended, moved = attention(queries, stretch_keys, stretch_values, segment_ids, block_live, moved)
    decode_keys, decode_values = place_pages(moved, inverse)
    projected = reduce_rows(attended, out_weight)
    return (attended, projected, decode_keys, decode_values)


def exchange(pieces, name):
    size = pieces.shape[0]
    me = lax.axis_index(name)
    total = lax.dynamic_index_in_dim(pieces, me, 0, keepdims=False).astype(jnp.float32)
    for shift in range(1, size):
        target = (me + shift) % size
        sent = lax.dynamic_index_in_dim(pieces, target, 0, keepdims=False).astype(jnp.bfloat16)
        pairs = [(i, (i + shift) % size) for i in range(size)]
        total = total + lax.ppermute(sent, name, pairs).astype(jnp.float32)
    return total


def reduce_rows(attended, out_weight):
    x_size, zl_size, c_size = [lax.axis_size(name) for name in HEAD]
    rows, width = attended.shape
    share = rows // (x_size * zl_size * c_size)
    order = attended.reshape(x_size, zl_size, c_size, share, width).transpose(2, 0, 1, 3, 4)
    columns = out_weight.shape[1]
    me = lax.axis_index("c")
    total = None
    for shift in range(c_size):
        rows_for = lax.dynamic_index_in_dim(order, (me + shift) % c_size, 0, keepdims=False)
        piece = jnp.dot(rows_for.reshape(-1, width), out_weight, preferred_element_type=jnp.float32)
        piece = piece.astype(jnp.bfloat16).reshape(x_size, zl_size, share, columns)
        if shift:
            pairs = [(i, (i + shift) % c_size) for i in range(c_size)]
            total = total + lax.ppermute(piece, "c", pairs).astype(jnp.float32)
        else:
            total = piece.astype(jnp.float32)
    total = exchange(total.reshape(x_size, zl_size, share, columns), "x")
    total = exchange(total.reshape(zl_size, share, columns), "zl")
    return total.astype(jnp.bfloat16)


def solution(mesh):
    seq_size, head_size = mesh.shape["seq"], mesh.shape["head"]
    fine = Mesh(mesh.devices.reshape(seq_size // 4, 4, head_size // 4, 2, 2), SEQ + HEAD)
    placed = (
        P(SEQ, HEAD),
        P(SEQ, HEAD),
        P(SEQ, HEAD),
        P(),
        P(),
        P(HEAD, None),
        P(None, SEQ, HEAD),
        P(None, SEQ, HEAD),
        P(),
    )
    return jax.shard_map(
        local,
        mesh=fine,
        in_specs=placed,
        out_specs=(
            P(SEQ, HEAD),
            P(SEQ + HEAD, None),
            P(None, SEQ, None, HEAD),
            P(None, SEQ, None, HEAD),
        ),
        check_vma=False,
    )
```

```python
import functools
import math

import jax
import jax.numpy as jnp
from jax import lax
from jax.experimental import pallas as pl
from jax.experimental.pallas import tpu as pltpu
from jax.sharding import Mesh
from jax.sharding import PartitionSpec as P

HD = 128
SEQ = ("zh", "y")
HEAD = ("x", "zl", "c")
Q_ROWS = 512


def relayout(cache_keys, cache_values, page_table):
    position = lax.axis_index(SEQ)
    groups = lax.axis_size(SEQ)
    layers, block_rows, feat_width = cache_keys.shape
    page_count = page_table.shape[0] // groups
    page_len = block_rows // page_count
    per_group = page_count // groups
    table = page_table.reshape(groups, groups, per_group)
    own = lax.dynamic_index_in_dim(table, position, 0, keepdims=False)
    run_ids = jnp.arange(groups, dtype=jnp.int32)
    goes = (own[:, 0] // page_count)[None, :] == run_ids[:, None]
    run_of = jnp.sum(jnp.where(goes, run_ids[None, :], 0), axis=1)
    send_pages = (run_of[:, None] * per_group + jnp.arange(per_group, dtype=jnp.int32)[None, :]).reshape(-1)
    both = jnp.stack([cache_keys, cache_values]).reshape(2, layers, page_count, page_len, feat_width)
    outgoing = jnp.take(both, send_pages, axis=2).reshape(2, layers, groups, per_group, page_len, feat_width)
    outgoing = outgoing.transpose(2, 0, 1, 3, 4, 5)
    hit = (table[:, :, 0] // page_count) == position
    slot_of = (jnp.sum(jnp.where(hit[:, :, None], table, 0), axis=1) % page_count).reshape(-1)
    arrivals = jnp.arange(page_count, dtype=jnp.int32)
    inverse = jnp.sum(jnp.where(slot_of[None, :] == arrivals[:, None], arrivals[None, :], 0), axis=1)
    return (outgoing, inverse)


def place_pages(outgoing, inverse):
    moved = lax.all_to_all(outgoing, SEQ, split_axis=0, concat_axis=0, tiled=True)
    _, kinds, layers, per_group, page_len, feat_width = moved.shape
    moved = moved.transpose(1, 2, 0, 3, 4, 5).reshape(kinds, layers, -1, page_len, feat_width)
    placed = jnp.take(moved, inverse, axis=2)
    return (placed[0], placed[1])


def attention_kernel(meta_ref, q_ref, qseg_ref, kseg_ref, k_ref, v_ref, o_ref, *, block_count, scale):
    chunk = pl.program_id(1)
    query_block = meta_ref[block_count]
    q = q_ref[...]
    qseg = qseg_ref[...]
    rows = q.shape[0]
    block_rows = k_ref.shape[1]
    local_pos = chunk * rows + lax.broadcasted_iota(jnp.int32, (rows, 1), 0)
    key_pos = lax.broadcasted_iota(jnp.int32, (1, block_rows), 1)

    def step(c, carry, allowed):
        row_best, weight_sum, numerator = carry
        s = lax.dot_general(q, k_ref[c], (((1,), (1,)), ((), ())), preferred_element_type=jnp.float32) * scale
        if allowed is not None:
            s = jnp.where(allowed, s, -jnp.inf)
        new_best = jnp.maximum(row_best, jnp.max(s, axis=1, keepdims=True))
        rescale = jnp.exp(row_best - new_best)
        w = jnp.exp(s - new_best)
        weight_sum = rescale * weight_sum + jnp.sum(w, axis=1, keepdims=True)
        added = jnp.dot(w.astype(jnp.bfloat16), v_ref[c], preferred_element_type=jnp.float32)
        return (new_best, weight_sum, rescale * numerator + added)

    initial = (
        jnp.full((rows, 1), -jnp.inf, jnp.float32),
        jnp.zeros((rows, 1), jnp.float32),
        jnp.zeros((rows, q.shape[1]), jnp.float32),
    )
    carry = step(query_block, initial, (qseg == kseg_ref[query_block]) & (key_pos <= local_pos))

    def body(c, carry):
        flag = meta_ref[c]
        return lax.cond(
            flag == 0,
            lambda x: x,
            lambda x: lax.cond(
                flag == 1,
                lambda y: step(c, y, qseg == kseg_ref[c]),
                lambda y: step(c, y, None),
                x,
            ),
            carry,
        )

    _, weight_sum, numerator = lax.fori_loop(0, query_block, body, carry)
    o_ref[...] = (numerator / weight_sum).astype(o_ref.dtype)


def attend(meta, queries, qseg, kseg, kv):
    block_count, _, block_rows, _ = kv.shape
    rows, feat_width = queries.shape
    kernel = functools.partial(attention_kernel, block_count=block_count, scale=1.0 / math.sqrt(HD))
    return pl.pallas_call(
        kernel,
        grid_spec=pltpu.PrefetchScalarGridSpec(
            num_scalar_prefetch=1,
            grid=(feat_width // HD, rows // Q_ROWS),
            in_specs=[
                pl.BlockSpec((Q_ROWS, HD), lambda h, i, meta: (i, h)),
                pl.BlockSpec((Q_ROWS, 1), lambda h, i, meta: (i, 0)),
                pl.BlockSpec((block_count, 1, block_rows), lambda h, i, meta: (0, 0, 0)),
                pl.BlockSpec((block_count, None, block_rows, HD), lambda h, i, meta: (0, 0, 0, h)),
                pl.BlockSpec((block_count, None, block_rows, HD), lambda h, i, meta: (0, 1, 0, h)),
            ],
            out_specs=pl.BlockSpec((Q_ROWS, HD), lambda h, i, meta: (i, h)),
        ),
        out_shape=jax.ShapeDtypeStruct((rows, feat_width), queries.dtype),
    )(meta, queries, qseg, kseg, kv, kv)


def stack_kernel(k_ref, v_ref, o_ref, sems):
    copies = [pltpu.make_async_copy(ref, o_ref.at[i], sems.at[i]) for i, ref in enumerate((k_ref, v_ref))]
    for copy in copies:
        copy.start()
    for copy in copies:
        copy.wait()


def stack_pair(first, second):
    anywhere = pl.BlockSpec(memory_space=pl.ANY)
    return pl.pallas_call(
        stack_kernel,
        in_specs=[anywhere, anywhere],
        out_specs=anywhere,
        scratch_shapes=[pltpu.SemaphoreType.DMA((2,))],
        out_shape=jax.ShapeDtypeStruct((2, *first.shape), first.dtype),
    )(first, second)


def attention(queries, stretch_keys, stretch_values, segment_ids, block_live, moved):
    position = lax.axis_index(SEQ)
    block_count = lax.axis_size(SEQ)
    block_rows, feat_width = queries.shape
    head_count = feat_width // HD
    seg_blocks = segment_ids.reshape(block_count, block_rows)
    query_seg = lax.dynamic_index_in_dim(seg_blocks, position, 0, keepdims=False)
    live_row = lax.dynamic_index_in_dim(block_live, position, 0, keepdims=False)
    block_ids = jnp.arange(block_count, dtype=jnp.int32)
    earlier = (block_ids < position) & (live_row == 1) & (seg_blocks[:, -1] >= query_seg[0])
    whole = earlier & (seg_blocks[:, 0] == query_seg[-1])
    flags = jnp.where(whole, 2, jnp.where(earlier, 1, 0)).astype(jnp.int32)
    meta = jnp.concatenate([flags, position.astype(jnp.int32)[None]])
    qseg = query_seg[:, None]
    kseg = seg_blocks[:, None, :]
    kv = stack_pair(stretch_keys, stretch_values)
    kv_all = lax.all_gather(kv, SEQ, axis=0, tiled=False)
    moved, kv_all = lax.optimization_barrier((moved, kv_all))
    return (attend(meta, queries, qseg, kseg, kv_all), moved)


def local(
    queries,
    stretch_keys,
    stretch_values,
    segment_ids,
    block_live,
    out_weight,
    cache_keys,
    cache_values,
    page_table,
):
    moved, inverse = relayout(cache_keys, cache_values, page_table)
    attended, moved = attention(queries, stretch_keys, stretch_values, segment_ids, block_live, moved)
    decode_keys, decode_values = place_pages(moved, inverse)
    projected = reduce_rows(attended, out_weight)
    return (attended, projected, decode_keys, decode_values)


def exchange(pieces, name):
    size = pieces.shape[0]
    me = lax.axis_index(name)
    total = lax.dynamic_index_in_dim(pieces, me, 0, keepdims=False).astype(jnp.float32)
    for shift in range(1, size):
        target = (me + shift) % size
        sent = lax.dynamic_index_in_dim(pieces, target, 0, keepdims=False).astype(jnp.bfloat16)
        pairs = [(i, (i + shift) % size) for i in range(size)]
        total = total + lax.ppermute(sent, name, pairs).astype(jnp.float32)
    return total


def reduce_rows(attended, out_weight):
    x_size, zl_size, c_size = [lax.axis_size(name) for name in HEAD]
    rows, width = attended.shape
    share = rows // (x_size * zl_size * c_size)
    order = attended.reshape(x_size, zl_size, c_size, share, width).transpose(2, 0, 1, 3, 4)
    columns = out_weight.shape[1]
    me = lax.axis_index("c")
    total = None
    for shift in range(c_size):
        rows_for = lax.dynamic_index_in_dim(order, (me + shift) % c_size, 0, keepdims=False)
        piece = jnp.dot(rows_for.reshape(-1, width), out_weight, preferred_element_type=jnp.float32)
        piece = piece.astype(jnp.bfloat16).reshape(x_size, zl_size, share, columns)
        if shift:
            pairs = [(i, (i + shift) % c_size) for i in range(c_size)]
            total = total + lax.ppermute(piece, "c", pairs).astype(jnp.float32)
        else:
            total = piece.astype(jnp.float32)
    total = exchange(total.reshape(x_size, zl_size, share, columns), "x")
    total = exchange(total.reshape(zl_size, share, columns), "zl")
    return total.astype(jnp.bfloat16)


def solution(mesh):
    seq_size, head_size = mesh.shape["seq"], mesh.shape["head"]
    fine = Mesh(mesh.devices.reshape(seq_size // 4, 4, head_size // 4, 2, 2), SEQ + HEAD)
    placed = (
        P(SEQ, HEAD),
        P(SEQ, HEAD),
        P(SEQ, HEAD),
        P(),
        P(),
        P(HEAD, None),
        P(None, SEQ, HEAD),
        P(None, SEQ, HEAD),
        P(),
    )
    return jax.shard_map(
        local,
        mesh=fine,
        in_specs=placed,
        out_specs=(
            P(SEQ, HEAD),
            P(SEQ + HEAD, None),
            P(None, SEQ, None, HEAD),
            P(None, SEQ, None, HEAD),
        ),
        check_vma=False,
    )
```
